128 devices in a mesh: angle: 8 (over z, core), row: 16 (over y, x).
Axes of the slice: x: 4, y: 4, z: 4, core: 2. Of those that a mesh axis runs over, the one named last changes fastest.
Arguments:
- measured: float32 [32, 256, 256], P('angle', 'row'), may hold values from -6 to 6
- bank: bfloat16 [8, 256, 256], replicated, may hold values from -0.09375 to 0.09375
- owner_tile: int32 [128, 64, 16], P(('angle', 'row')), may hold values from 0 to 127, all different within a row; in each aligned block of 64 rows (0 to 63, 64 to 127, ..., all dimensions but the last counted through in order) at most 16 rows name the same one
- line_index: int32 [128, 64, 16], P(('angle', 'row')), may hold values from 0 to 1023
- block_index: int32 [128, 1024, 1], P(('angle', 'row')), may hold values from 0 to 7; in each aligned block of 1024 rows (0 to 1023, 1024 to 2047, ..., all dimensions but the last counted through in order) at most 256 rows name the same one
- dual_w1: float32 [2, 3, 16, 7], replicated, may hold values from -1.25 to 1.25
- dual_b1: float32 [2, 16], replicated, may hold values from -3 to 3
- dual_w2: float32 [2, 5, 16], replicated, may hold values from -1.5 to 1.5
- primal_w1: float32 [2, 3, 16, 6], replicated, may hold values from -1.5 to 1.5
- primal_b1: float32 [2, 16], replicated, may hold values from -3 to 3
- primal_w2: float32 [2, 5, 16], replicated, may hold values from -1.5 to 1.5
Outputs:
- primal_state: float32 [512, 256, 5, 256], P(('angle', 'row'))
- dual_state: float32 [32, 256, 5, 256], P('angle', 'row')
The draws below stay inside these ranges and needn't reach their ends.
Inputs may be any that keep to these rules, and one draw needn't show every extreme that they name: `owner_tile`: each ray row lists 16 different slabs; the 64 ray rows of one group name any one slab at most 16 times, a bound that some block reaches. `block_index`: the 1024 pairs of one group name any one block kind at most 256 times, a bound that some group reaches.
All inputs are finite; a program needn't handle non-finite values.
Results may differ from the reference program's by a relative error of at most 0.00095.
Values may be sent and summed in bfloat16 or wider, within the bound.
No kernel may reach another device: no remote copies, remote signals or barrier semaphores. Data moves between devices by JAX's collectives and lax.ppermute only.
A program may use at most 192 MiB of HBM per device.

```python
import math
import jax
import jax.numpy as jnp
import numpy as np
from jax import lax

DCOLS = 256
NX = 256
NY = 256
CH = 5
HID = 16
NB = 8
K = 16
ITERS = 2
DROW_DEV = 16
VIEW_DEV = 4
NOWNERS = 128
RT = 64
CAP = 16
BCAP = 256
LPD = 1024
VIEWS = 32
DROWS = 256
NZ = 512


def set_ends(drawn, stream_key, low, high):
    shape = drawn.shape
    spot = [jax.random.randint(jax.random.fold_in(stream_key, axis), (), 0, shape[axis]) for axis in range(len(shape))]
    drawn = drawn.at[tuple(spot)].set(low)
    longest = shape.index(max(shape))
    spot[longest] = (spot[longest] + 1) % shape[longest]
    return drawn.at[tuple(spot)].set(high)


def levels(stream_key, extent, split, low, high):
    def one(axis_at, blocks):
        heights = jax.random.uniform(jax.random.fold_in(jax.random.fold_in(stream_key, 6), axis_at), (blocks,), jnp.float32, low / len(split), high / len(split))
        return jnp.repeat(jnp.exp(heights), extent[axis_at] // blocks).reshape((-1,) + (1,) * (len(extent) - axis_at - 1))

    factor_of = one(*split[0])
    for cut in split[1:]:
        factor_of = factor_of * one(*cut)
    return factor_of


def assign_block(key, own, number, rows, number_of, top, most, slope):
    ranking = jax.random.permutation(key, number_of)
    crowded, ordinary = shares(number_of, rows * top, most, slope, True), shares(number_of, rows * top, most, slope, False)
    places = jnp.arange(number_of)

    def named(lengths, turn):
        used = int((lengths > 0).sum())
        fixed = max(1, used // 4)
        moved = fixed + (places - fixed + turn * (used - fixed)) % max(1, number_of - fixed)
        return jnp.zeros((number_of,), jnp.int32).at[ranking[jnp.where(places < fixed, places, moved)]].set(jnp.asarray(lengths, jnp.int32))

    lengths = jnp.where(number % 4 == 0, named(crowded, number // 4), named(ordinary, number - number // 4 - 1))
    mixed = jax.random.permutation(jax.random.fold_in(own, 3), number_of)
    giver, receiver = mixed[0:number_of // 2 * 2:2], mixed[1:number_of // 2 * 2:2]
    room = jnp.minimum(lengths[giver] - 1, most - lengths[receiver]) // 2
    room = jnp.where((giver == ranking[0]) | (receiver == ranking[0]) | (lengths[receiver] == 0), 0, jnp.maximum(room, 0))
    moved = jax.random.randint(jax.random.fold_in(own, 4), (number_of // 2,), 0, 1 << 20) % (room + 1)
    lengths = lengths.at[giver].add(-moved).at[receiver].add(moved)
    items = jnp.searchsorted(jnp.cumsum(lengths), jnp.arange(rows * top), side="right").astype(jnp.int32)
    table = items.reshape(top, rows).T
    table = table[jax.random.permutation(jax.random.fold_in(own, 1), rows)]
    turn = jax.random.randint(jax.random.fold_in(own, 2), (rows, 1), 0, top)
    return jnp.take_along_axis(table, (jnp.arange(top)[None, :] + turn) % top, axis=1)


def shares(number_of, total, most, slope, full):
    portions = [(1 << 20) // math.isqrt(standing ** slope) + 1 for standing in range(1, number_of + 1)]
    largest = most if full else min(most, max(-(-total // number_of), total * portions[0] // sum(portions)))
    least = 1 if total - largest >= number_of - 1 else 0
    counts, rest = [largest] + [least] * (number_of - 1), total - largest - least * (number_of - 1)
    while rest > 0:
        free = [i for i in range(1, number_of) if counts[i] < largest] or [i for i in range(1, number_of) if counts[i] < most]
        mass, left = sum([portions[i] for i in free]), rest
        for i in free:
            addition = min(most - counts[i], max(1, left * portions[i] // mass), rest)
            counts[i] = counts[i] + addition
            rest = rest - addition
    return np.array(counts)


def gaussian(stream_key, shape, scale, reach, shards=(), held_as=jnp.bfloat16):
    drawn = jax.random.normal(stream_key, shape, jnp.float32) * scale
    if len(shards) > 0:
        drawn = levels(stream_key, shape, shards, -0.22, 0.18) * drawn
    return jnp.clip(drawn, min=-reach, max=reach).astype(held_as)


def setup_inputs(seed: int = 0) -> dict:
    seeds = jax.random.split(jax.random.key(seed), 12)
    measured = gaussian(seeds[0], (VIEWS, DROWS, DCOLS), 1.0, 6.0, ((0, 8), (1, 16)), jnp.float32)
    bank = gaussian(seeds[1], (NB, DCOLS, NX), (NX * K) ** -0.5, 0.09375)
    owner_tile_keys = jax.random.split(jax.random.fold_in(seeds[2], 1), NOWNERS * RT // RT)
    owner_tile_turns = jax.random.permutation(jax.random.fold_in(seeds[2], 3), NOWNERS * RT // RT)
    owner_tile = jax.vmap(lambda own, number: assign_block(jax.random.fold_in(seeds[2], 2), own, number, RT, NOWNERS, K, CAP, 2))(owner_tile_keys, owner_tile_turns).reshape((NOWNERS, RT, K))
    line_index = set_ends(jax.random.randint(seeds[3], (NOWNERS, RT, K), 0, LPD), jax.random.fold_in(seeds[3], 1), 0, LPD - 1).astype(jnp.int32)
    block_index_keys = jax.random.split(jax.random.fold_in(seeds[4], 1), NOWNERS * (RT * K) // (RT * K))
    block_index_turns = jax.random.permutation(jax.random.fold_in(seeds[4], 3), NOWNERS * (RT * K) // (RT * K))
    block_index = jax.vmap(lambda own, number: assign_block(jax.random.fold_in(seeds[4], 2), own, number, RT * K, NB, 1, BCAP, 1))(block_index_keys, block_index_turns).reshape((NOWNERS, RT * K, 1))
    dual_w1 = gaussian(seeds[5], (ITERS, 3, HID, CH + 2), (3 * (CH + 2)) ** -0.5, 1.25, (), jnp.float32)
    dual_b1 = gaussian(seeds[6], (ITERS, HID), 0.5, 3.0, (), jnp.float32)
    dual_w2 = gaussian(seeds[7], (ITERS, CH, HID), HID ** -0.5, 1.5, (), jnp.float32)
    primal_w1 = gaussian(seeds[8], (ITERS, 3, HID, CH + 1), (3 * (CH + 1)) ** -0.5, 1.5, (), jnp.float32)
    primal_b1 = gaussian(seeds[9], (ITERS, HID), 0.5, 3.0, (), jnp.float32)
    primal_w2 = gaussian(seeds[10], (ITERS, CH, HID), HID ** -0.5, 1.5, (), jnp.float32)
    return {"measured": measured, "bank": bank, "owner_tile": owner_tile, "line_index": line_index, "block_index": block_index, "dual_w1": dual_w1, "dual_b1": dual_b1, "dual_w2": dual_w2, "primal_w1": primal_w1, "primal_b1": primal_b1, "primal_w2": primal_w2}


highest = lax.Precision.HIGHEST


def conv_taps(padded, weights, length):
    running = jnp.einsum("oi,abic->aboc", weights[0], padded[0:length], precision=highest)
    running = running + jnp.einsum("oi,abic->aboc", weights[1], padded[1:length + 1], precision=highest)
    running = running + jnp.einsum("oi,abic->aboc", weights[2], padded[2:length + 2], precision=highest)
    return running


def dual_net(dual_state, projected, measured, weights_in, biases, weights_out):
    stacked = jnp.concatenate([dual_state, projected[:, :, None, :], measured[:, :, None, :]], axis=2)
    row_major = jnp.moveaxis(stacked, 1, 0)

    def one_row(columns):
        padded = jnp.pad(columns, ((1, 1), (0, 0), (0, 0)))[:, None]
        hidden = jax.nn.relu(conv_taps(padded, weights_in, VIEWS) + biases[None, None, :, None])
        return jnp.einsum("oh,abhc->aboc", weights_out, hidden, precision=highest)[:, 0]

    change = lax.map(one_row, row_major)
    return dual_state + jnp.moveaxis(change, 0, 1)


def primal_net(primal_state, back, weights_in, biases, weights_out):
    stacked = jnp.concatenate([primal_state, back[:, :, None, :]], axis=2)
    row_major = jnp.moveaxis(stacked, 1, 0)

    def one_row(columns):
        padded = jnp.pad(columns, ((1, 1), (0, 0), (0, 0)))[:, None]
        hidden = jax.nn.relu(conv_taps(padded, weights_in, NZ) + biases[None, None, :, None])
        return jnp.einsum("oh,abhc->aboc", weights_out, hidden, precision=highest)[:, 0]

    change = lax.map(one_row, row_major)
    return primal_state + jnp.moveaxis(change, 0, 1)


def to_rows(sinogram):
    shaped = sinogram.reshape(NOWNERS // (DROWS // DROW_DEV), VIEW_DEV, DROWS // DROW_DEV, DROW_DEV, DCOLS)
    return jnp.transpose(shaped, (0, 2, 1, 3, 4)).reshape(NOWNERS * RT, DCOLS)


def from_rows(ray_rows):
    shaped = ray_rows.reshape(NOWNERS // (DROWS // DROW_DEV), DROWS // DROW_DEV, VIEW_DEV, DROW_DEV, DCOLS)
    return jnp.transpose(shaped, (0, 2, 1, 3, 4)).reshape(VIEWS, DROWS, DCOLS)


def reference(measured, bank, owner_tile, line_index, block_index, dual_w1, dual_b1, dual_w2, primal_w1, primal_b1, primal_w2):
    global_line = (owner_tile * LPD + line_index).reshape(-1).astype(jnp.int32)
    block_flat = block_index.reshape(-1).astype(jnp.int32)
    block_rows = block_index.reshape(NOWNERS * RT, K).astype(jnp.int32)
    flat_bank = jnp.transpose(bank, (1, 0, 2)).reshape(DCOLS, NB * NX)
    dual_state = jnp.zeros((VIEWS, DROWS, CH, DCOLS), jnp.float32)
    primal_state = jnp.zeros((NZ, NY, CH, NX), jnp.float32)
    for iteration in range(ITERS):
        if iteration == 0:
            projected = jnp.zeros((VIEWS, DROWS, DCOLS), jnp.float32)
        else:
            volume_lines = primal_state[:, :, 1, :].reshape(NZ * NY, NX).astype(jnp.bfloat16)

            def add_block(number, running):
                matrix = lax.dynamic_index_in_dim(bank, number, 0, keepdims=False)
                image = lax.dot_general(volume_lines, matrix, (((1,), (1,)), ((), ())), preferred_element_type=jnp.float32)
                return running + jnp.where((block_flat == number)[:, None], image[global_line], jnp.float32(0.0))

            running = lax.fori_loop(0, NB, add_block, jnp.zeros((NOWNERS * RT * K, DCOLS), jnp.float32))
            projected = from_rows(running.reshape(NOWNERS * RT, K, DCOLS).sum(axis=1))
        dual_state = dual_net(dual_state, projected, measured, dual_w1[iteration], dual_b1[iteration], dual_w2[iteration])
        sino_rows = to_rows(dual_state[:, :, 0, :]).astype(jnp.bfloat16)
        all_blocks = jnp.dot(sino_rows, flat_bank, preferred_element_type=jnp.float32).reshape(NOWNERS * RT, NB, NX)
        picked = jnp.take_along_axis(all_blocks, block_rows[:, :, None], axis=1)
        pieces = lax.optimization_barrier(picked.astype(jnp.bfloat16).reshape(NOWNERS * RT * K, NX))
        back = jnp.zeros((NZ * NY, NX), jnp.float32).at[global_line].add(pieces.astype(jnp.float32))
        primal_state = primal_net(primal_state, back.reshape(NZ, NY, NX), primal_w1[iteration], primal_b1[iteration], primal_w2[iteration])
    return primal_state, dual_state
```

```python
import functools

import jax
import jax.numpy as jnp
from jax import lax
from jax.experimental import pallas as pl
from jax.experimental.pallas import tpu as pltpu
from jax.sharding import PartitionSpec as P

NY = 256
CH = 5
ITERS = 2
SLAB_DEV = 4
YB = 32


highest = lax.Precision.HIGHEST


def extended(block, sides, width):
    for axis, dim in sides:
        count = lax.axis_size(axis)
        forward = [(i, i + 1) for i in range(count - 1)]
        backward = [(target, source) for source, target in forward]
        low = lax.ppermute(
            lax.slice_in_dim(block, block.shape[dim] - width, None, axis=dim), axis, forward
        )
        high = lax.ppermute(lax.slice_in_dim(block, 0, width, axis=dim), axis, backward)
        block = jnp.concatenate([low, block, high], axis=dim)
    return block


def shift_pair(low_src, high_src, axis):
    count = lax.axis_size(axis)
    forward = [(i, i + 1) for i in range(count - 1)]
    backward = [(target, source) for source, target in forward]
    low = lax.ppermute(low_src, axis, forward)
    high = lax.ppermute(high_src, axis, backward)
    return low, high


def conv_taps(padded, weights, length):
    running = jnp.einsum("oi,abic->aboc", weights[0], padded[0:length], precision=highest)
    running = running + jnp.einsum(
        "oi,abic->aboc", weights[1], padded[1 : length + 1], precision=highest
    )
    running = running + jnp.einsum(
        "oi,abic->aboc", weights[2], padded[2 : length + 2], precision=highest
    )
    return running


def mix_update(states, hidden, weights):
    return states + jnp.einsum("oh,abhc->aboc", weights, hidden, precision=highest)


def exclusive_slots(labels, count):
    member = (labels[:, None] == jnp.arange(count, dtype=jnp.int32)[None, :]).astype(jnp.int32)
    return jnp.sum((jnp.cumsum(member, axis=0) - member) * member, axis=1)


def primal_kernel(full, hid, w1_ref, b1_ref, w2_ref, *refs):
    if full:
        s_ref, b_ref, los_ref, lob_ref, his_ref, hib_ref, o_ref = refs
    else:
        b_ref, lob_ref, hib_ref, o_ref = refs
    nz = b_ref.shape[0]
    yb = b_ref.shape[1]
    nin = CH + 1

    def plane(zz, c, ys, xs):
        if c == CH:
            if zz < 0:
                return lob_ref[pl.ds(ys, 8), pl.ds(xs, 128)]
            if zz >= nz:
                return hib_ref[pl.ds(ys, 8), pl.ds(xs, 128)]
            return b_ref[zz, pl.ds(ys, 8), pl.ds(xs, 128)]
        if zz < 0:
            return los_ref[c, pl.ds(ys, 8), pl.ds(xs, 128)]
        if zz >= nz:
            return his_ref[c, pl.ds(ys, 8), pl.ds(xs, 128)]
        return s_ref[zz, c, pl.ds(ys, 8), pl.ds(xs, 128)]

    chans = list(range(CH + 1)) if full else [CH]
    for z in range(nz):

        def body(i, carry):
            ys = pl.multiple_of((i // 2) * 8, 8)
            xs = pl.multiple_of((i % 2) * 128, 128)
            inputs = [
                (t, c, plane(z + t - 1, c, ys, xs)) for t in range(3) for c in chans
            ]
            change = [None] * CH
            for h in range(hid):
                acc = None
                for t, c, value in inputs:
                    term = w1_ref[(t * hid + h) * nin + c] * value
                    acc = term if acc is None else acc + term
                acc = jnp.maximum(acc + b1_ref[h], 0.0)
                for c in range(CH):
                    term = w2_ref[c * hid + h] * acc
                    change[c] = term if change[c] is None else change[c] + term
            for c in range(CH):
                if full:
                    out = s_ref[z, c, pl.ds(ys, 8), pl.ds(xs, 128)] + change[c]
                else:
                    out = change[c]
                o_ref[z, c, pl.ds(ys, 8), pl.ds(xs, 128)] = out
            return carry

        lax.fori_loop(0, (yb // 8) * 2, body, 0)


def primal_step(state, back, lo_s, lo_b, hi_s, hi_b, w1, b1, w2):
    nz, ny, nx = back.shape
    hid = b1.shape[0]
    full = state is not None
    smem = pl.BlockSpec(memory_space=pltpu.SMEM)
    spec_s = pl.BlockSpec((nz, CH, YB, nx), lambda j: (0, 0, j, 0))
    spec_b = pl.BlockSpec((nz, YB, nx), lambda j: (0, j, 0))
    spec_hs = pl.BlockSpec((CH, YB, nx), lambda j: (0, j, 0))
    spec_hb = pl.BlockSpec((YB, nx), lambda j: (j, 0))
    if full:
        operands = (state, back, lo_s, lo_b, hi_s, hi_b)
        specs = [spec_s, spec_b, spec_hs, spec_hb, spec_hs, spec_hb]
    else:
        operands = (back, lo_b, hi_b)
        specs = [spec_b, spec_hb, spec_hb]
    return pl.pallas_call(
        functools.partial(primal_kernel, full, hid),
        grid=(ny // YB,),
        in_specs=[smem, smem, smem] + specs,
        out_specs=spec_s,
        out_shape=jax.ShapeDtypeStruct((nz, CH, ny, nx), jnp.float32),
        compiler_params=pltpu.CompilerParams(dimension_semantics=("arbitrary",)),
    )(w1.reshape(-1), b1, w2.reshape(-1), *operands)


def local(
    measured,
    bank,
    owner_tile,
    line_index,
    block_index,
    dual_w1,
    dual_b1,
    dual_w2,
    primal_w1,
    primal_b1,
    primal_w2,
):
    view_dev, drow_dev, dcols = measured.shape
    blocks = bank.shape[0]
    width = bank.shape[2]
    per_row = owner_tile.shape[2]
    angle_count = lax.axis_size("angle")
    row_count = lax.axis_size("row")
    owners = angle_count * row_count
    ray_rows = view_dev * drow_dev
    pair_count = ray_rows * per_row
    capacity = 2 * pair_count // owners
    slots = owners * capacity
    lines_dev = SLAB_DEV * NY
    both = ("angle", "row")
    owner_flat = owner_tile.reshape(-1)
    line_flat = line_index.reshape(-1)
    block_flat = block_index.reshape(-1)
    slot_flat = exclusive_slots(owner_flat, owners)
    dest = owner_flat * capacity + slot_flat
    pair_ids = jnp.arange(pair_count, dtype=jnp.int32)
    row_block = (pair_ids // per_row) * blocks + block_flat

    slot_ids = jnp.arange(slots, dtype=jnp.int32)
    hit = dest[None, :] == slot_ids[:, None]
    ids_send = jnp.sum(jnp.where(hit, line_flat[None, :] + 1, 0), axis=1) - 1
    slot_rb = jnp.sum(jnp.where(hit, row_block[None, :] + 1, 0), axis=1) - 1
    gsel = (
        slot_rb[None, :] == jnp.arange(ray_rows * blocks, dtype=jnp.int32)[:, None]
    ).astype(jnp.bfloat16)
    arrived_ids = lax.all_to_all(
        ids_send.reshape(owners, capacity), both, split_axis=0, concat_axis=0, tiled=True
    ).reshape(-1)
    rsel = (
        arrived_ids[:, None] == jnp.arange(lines_dev, dtype=jnp.int32)[None, :]
    ).astype(jnp.bfloat16)

    flat_bank = jnp.transpose(bank, (1, 0, 2)).reshape(dcols, blocks * width)
    bank_t = jnp.transpose(bank, (0, 2, 1)).reshape(blocks * width, dcols).astype(jnp.float32)

    def forward(volume_lines):
        chosen = jnp.dot(rsel, volume_lines, preferred_element_type=jnp.float32).astype(
            jnp.bfloat16
        )
        returned = lax.all_to_all(
            chosen.reshape(owners, capacity, width), both, split_axis=0, concat_axis=0, tiled=True
        ).reshape(slots, width)
        summed = jnp.dot(gsel, returned, preferred_element_type=jnp.float32)
        rays = jnp.dot(
            summed.reshape(ray_rows, blocks * width), bank_t, precision=highest
        )
        return rays.reshape(view_dev, drow_dev, dcols)

    def backward(sino_rows):
        all_blocks = jnp.dot(sino_rows, flat_bank, preferred_element_type=jnp.float32).astype(
            jnp.bfloat16
        )
        outgoing = lax.dot_general(
            gsel,
            all_blocks.reshape(ray_rows * blocks, width),
            (((0,), (0,)), ((), ())),
            preferred_element_type=jnp.float32,
        ).astype(jnp.bfloat16)
        arrived = lax.all_to_all(
            outgoing.reshape(owners, capacity, width), both, split_axis=0, concat_axis=0, tiled=True
        ).reshape(slots, width)
        back = lax.dot_general(
            rsel, arrived, (((0,), (0,)), ((), ())), preferred_element_type=jnp.float32
        )
        return back.reshape(SLAB_DEV, NY, width)

    dual_state = jnp.zeros((view_dev, drow_dev, CH, dcols), jnp.float32)
    state = None
    for iteration in range(ITERS):
        if iteration == 0:
            projected = jnp.zeros((view_dev, drow_dev, dcols), jnp.float32)
        else:
            volume_lines = state[:, 1].reshape(lines_dev, width).astype(jnp.bfloat16)
            projected = forward(volume_lines)
        stacked = jnp.concatenate(
            [dual_state, projected[:, :, None, :], measured[:, :, None, :]], axis=2
        )
        padded = extended(stacked, (("angle", 0),), 1)
        hidden = jax.nn.relu(
            conv_taps(padded, dual_w1[iteration], view_dev)
            + dual_b1[iteration][None, None, :, None]
        )
        dual_state = mix_update(dual_state, hidden, dual_w2[iteration])
        sino_rows = dual_state[:, :, 0, :].reshape(ray_rows, dcols).astype(jnp.bfloat16)
        back = backward(sino_rows)
        lo_b, hi_b = shift_pair(back[-1], back[0], both)
        if state is None:
            state = primal_step(
                None, back, None, lo_b, None, hi_b,
                primal_w1[iteration], primal_b1[iteration], primal_w2[iteration],
            )
        else:
            lo_s, hi_s = shift_pair(state[-1], state[0], both)
            state = primal_step(
                state, back, lo_s, lo_b, hi_s, hi_b,
                primal_w1[iteration], primal_b1[iteration], primal_w2[iteration],
            )
    primal_state = jnp.transpose(state, (0, 2, 1, 3))
    return (primal_state, dual_state)


def solution(mesh):
    placed = (
        P("angle", "row", None),
        P(),
        P(("angle", "row"), None, None),
        P(("angle", "row"), None, None),
        P(("angle", "row"), None, None),
        P(),
        P(),
        P(),
        P(),
        P(),
        P(),
    )
    return jax.shard_map(
        local,
        mesh=mesh,
        in_specs=placed,
        out_specs=(P(("angle", "row"), None, None, None), P("angle", "row", None, None)),
        check_vma=False,
    )
```

```python
import functools

import jax
import jax.numpy as jnp
from jax import lax
from jax.experimental import pallas as pl
from jax.experimental.pallas import tpu as pltpu
from jax.sharding import PartitionSpec as P

NY = 256
CH = 5
ITERS = 2
SLAB_DEV = 4
YB = 32


highest = lax.Precision.HIGHEST


def extended(block, sides, width):
    for axis, dim in sides:
        count = lax.axis_size(axis)
        forward = [(i, i + 1) for i in range(count - 1)]
        backward = [(target, source) for source, target in forward]
        low = lax.ppermute(
            lax.slice_in_dim(block, block.shape[dim] - width, None, axis=dim), axis, forward
        )
        high = lax.ppermute(lax.slice_in_dim(block, 0, width, axis=dim), axis, backward)
        block = jnp.concatenate([low, block, high], axis=dim)
    return block


def shift_pair(low_src, high_src, axis):
    count = lax.axis_size(axis)
    forward = [(i, i + 1) for i in range(count - 1)]
    backward = [(target, source) for source, target in forward]
    low = lax.ppermute(low_src, axis, forward)
    high = lax.ppermute(high_src, axis, backward)
    return low, high


def conv_taps(padded, weights, length):
    running = jnp.einsum("oi,abic->aboc", weights[0], padded[0:length], precision=highest)
    running = running + jnp.einsum(
        "oi,abic->aboc", weights[1], padded[1 : length + 1], precision=highest
    )
    running = running + jnp.einsum(
        "oi,abic->aboc", weights[2], padded[2 : length + 2], precision=highest
    )
    return running


def mix_update(states, hidden, weights):
    return states + jnp.einsum("oh,abhc->aboc", weights, hidden, precision=highest)


def exclusive_slots(labels, count):
    member = (labels[:, None] == jnp.arange(count, dtype=jnp.int32)[None, :]).astype(jnp.int32)
    return jnp.sum((jnp.cumsum(member, axis=0) - member) * member, axis=1)


def primal_kernel(full, hid, rows, nlo, outs, w1_ref, b1_ref, w2_ref, f_ref, *refs):
    if full:
        s_ref, b_ref, lob_ref, hib_ref, o_ref = refs
    else:
        b_ref, lob_ref, hib_ref, o_ref = refs
    nz = b_ref.shape[0]
    yb = b_ref.shape[1]
    nx = b_ref.shape[2]
    nin = CH + 1

    def plane(zz, c, ys):
        if c == CH:
            if zz < 0:
                return lob_ref[zz + nlo, pl.ds(ys, rows), :]
            if zz >= nz:
                return hib_ref[zz - nz, pl.ds(ys, rows), :]
            return b_ref[zz, pl.ds(ys, rows), :]
        return s_ref[zz + 1, c, pl.ds(ys, rows), :]

    chans = list(range(CH + 1)) if full else [CH]
    for slot, z in enumerate(outs):

        def body(i, carry):
            ys = pl.multiple_of(i * rows, rows)
            inputs = [(t, c, plane(z + t - 1, c, ys)) for t in range(3) for c in chans]
            change = [None] * CH
            for h in range(hid):
                acc = None
                for t, c, value in inputs:
                    term = w1_ref[(t * hid + h) * nin + c] * value
                    acc = term if acc is None else acc + term
                acc = jnp.maximum(acc + b1_ref[h], 0.0)
                for c in range(CH):
                    term = w2_ref[c * hid + h] * acc
                    change[c] = term if change[c] is None else change[c] + term
            for c in range(CH):
                if full:
                    out = s_ref[z + 1, c, pl.ds(ys, rows), :] + change[c]
                elif z < 0:
                    out = change[c] * f_ref[0]
                elif z >= nz:
                    out = change[c] * f_ref[1]
                else:
                    out = change[c]
                o_ref[slot, c, pl.ds(ys, rows), :] = out
            return carry

        lax.fori_loop(0, yb // rows, body, 0)


def primal_step(state, back, lo_b, hi_b, flags, w1, b1, w2):
    nz, ny, nx = back.shape
    nlo = lo_b.shape[0]
    hid = b1.shape[0]
    full = state is not None
    if full:
        outs = tuple(range(nz))
        rows = 8
    else:
        outs = tuple(range(-1, nz + 1))
        rows = 16
    smem = pl.BlockSpec(memory_space=pltpu.SMEM)
    spec_s = pl.BlockSpec((nz + 2, CH, YB, nx), lambda j: (0, 0, j, 0))
    spec_b = pl.BlockSpec((nz, YB, nx), lambda j: (0, j, 0))
    spec_h = pl.BlockSpec((nlo, YB, nx), lambda j: (0, j, 0))
    spec_o = pl.BlockSpec((len(outs), CH, YB, nx), lambda j: (0, 0, j, 0))
    operands = (back, lo_b, hi_b)
    specs = [spec_b, spec_h, spec_h]
    if full:
        operands = (state,) + operands
        specs = [spec_s] + specs
    return pl.pallas_call(
        functools.partial(primal_kernel, full, hid, rows, nlo, outs),
        grid=(ny // YB,),
        in_specs=[smem, smem, smem, smem] + specs,
        out_specs=spec_o,
        out_shape=jax.ShapeDtypeStruct((len(outs), CH, ny, nx), jnp.float32),
        compiler_params=pltpu.CompilerParams(dimension_semantics=("arbitrary",)),
    )(w1.reshape(-1), b1, w2.reshape(-1), flags, *operands)


def local(
    measured,
    bank,
    owner_tile,
    line_index,
    block_index,
    dual_w1,
    dual_b1,
    dual_w2,
    primal_w1,
    primal_b1,
    primal_w2,
):
    view_dev, drow_dev, dcols = measured.shape
    blocks = bank.shape[0]
    width = bank.shape[2]
    per_row = owner_tile.shape[2]
    angle_count = lax.axis_size("angle")
    row_count = lax.axis_size("row")
    owners = angle_count * row_count
    ray_rows = view_dev * drow_dev
    pair_count = ray_rows * per_row
    capacity = 2 * pair_count // owners
    slots = owners * capacity
    lines_dev = SLAB_DEV * NY
    both = ("angle", "row")
    owner_flat = owner_tile.reshape(-1)
    line_flat = line_index.reshape(-1)
    block_flat = block_index.reshape(-1)
    slot_flat = exclusive_slots(owner_flat, owners)
    dest = owner_flat * capacity + slot_flat
    pair_ids = jnp.arange(pair_count, dtype=jnp.int32)
    row_block = (pair_ids // per_row) * blocks + block_flat

    slot_ids = jnp.arange(slots, dtype=jnp.int32)
    hit = dest[None, :] == slot_ids[:, None]
    ids_send = jnp.sum(jnp.where(hit, line_flat[None, :] + 1, 0), axis=1) - 1
    slot_rb = jnp.sum(jnp.where(hit, row_block[None, :] + 1, 0), axis=1) - 1
    gsel = (
        slot_rb[None, :] == jnp.arange(ray_rows * blocks, dtype=jnp.int32)[:, None]
    ).astype(jnp.bfloat16)
    arrived_ids = lax.all_to_all(
        ids_send.reshape(owners, capacity), both, split_axis=0, concat_axis=0, tiled=True
    ).reshape(-1)
    rsel = (
        arrived_ids[:, None] == jnp.arange(lines_dev, dtype=jnp.int32)[None, :]
    ).astype(jnp.bfloat16)
    rsel_t = (
        arrived_ids[None, :] == jnp.arange(lines_dev, dtype=jnp.int32)[:, None]
    ).astype(jnp.bfloat16)
    place = lax.axis_index(both)
    flags = jnp.stack([place > 0, place < owners - 1]).astype(jnp.float32)

    flat_bank = jnp.transpose(bank, (1, 0, 2)).reshape(dcols, blocks * width)
    bank_t = jnp.transpose(bank, (0, 2, 1)).reshape(blocks * width, dcols).astype(jnp.float32)

    def forward(volume_lines):
        chosen = jnp.dot(rsel, volume_lines, preferred_element_type=jnp.float32).astype(
            jnp.bfloat16
        )
        returned = lax.all_to_all(
            chosen.reshape(owners, capacity, width), both, split_axis=0, concat_axis=0, tiled=True
        ).reshape(slots, width)
        summed = jnp.dot(gsel, returned, preferred_element_type=jnp.float32)
        rays = jnp.dot(
            summed.reshape(ray_rows, blocks * width), bank_t, precision=highest
        )
        return rays.reshape(view_dev, drow_dev, dcols)

    def backward(sino_rows):
        all_blocks = jnp.dot(sino_rows, flat_bank, preferred_element_type=jnp.float32).astype(
            jnp.bfloat16
        )
        outgoing = lax.dot_general(
            gsel,
            all_blocks.reshape(ray_rows * blocks, width),
            (((0,), (0,)), ((), ())),
            preferred_element_type=jnp.float32,
        ).astype(jnp.bfloat16)
        arrived = lax.all_to_all(
            outgoing.reshape(owners, capacity, width), both, split_axis=0, concat_axis=0, tiled=True
        ).reshape(slots, width)
        back = jnp.dot(rsel_t, arrived, preferred_element_type=jnp.float32)
        return back.reshape(SLAB_DEV, NY, width)

    dual_state = jnp.zeros((view_dev, drow_dev, CH, dcols), jnp.float32)
    state = None
    for iteration in range(ITERS):
        if iteration == 0:
            projected = jnp.zeros((view_dev, drow_dev, dcols), jnp.float32)
        else:
            volume_lines = state[1:-1, 1].reshape(lines_dev, width).astype(jnp.bfloat16)
            projected = forward(volume_lines)
        stacked = jnp.concatenate(
            [dual_state, projected[:, :, None, :], measured[:, :, None, :]], axis=2
        )
        padded = extended(stacked, (("angle", 0),), 1)
        hidden = jax.nn.relu(
            conv_taps(padded, dual_w1[iteration], view_dev)
            + dual_b1[iteration][None, None, :, None]
        )
        dual_state = mix_update(dual_state, hidden, dual_w2[iteration])
        sino_rows = dual_state[:, :, 0, :].reshape(ray_rows, dcols).astype(jnp.bfloat16)
        back = backward(sino_rows)
        if state is None:
            lo_b, hi_b = shift_pair(back[-2:], back[:2], both)
            state = primal_step(
                None, back, lo_b, hi_b, flags,
                primal_w1[iteration], primal_b1[iteration], primal_w2[iteration],
            )
        else:
            lo_b, hi_b = shift_pair(back[-1:], back[:1], both)
            state = primal_step(
                state, back, lo_b, hi_b, flags,
                primal_w1[iteration], primal_b1[iteration], primal_w2[iteration],
            )
    primal_state = jnp.transpose(state, (0, 2, 1, 3))
    return (primal_state, dual_state)


def solution(mesh):
    placed = (
        P("angle", "row", None),
        P(),
        P(("angle", "row"), None, None),
        P(("angle", "row"), None, None),
        P(("angle", "row"), None, None),
        P(),
        P(),
        P(),
        P(),
        P(),
        P(),
    )
    return jax.shard_map(
        local,
        mesh=mesh,
        in_specs=placed,
        out_specs=(P(("angle", "row"), None, None, None), P("angle", "row", None, None)),
        check_vma=False,
    )
```

```python
import functools

import jax
import jax.numpy as jnp
from jax import lax
from jax.experimental import pallas as pl
from jax.experimental.pallas import tpu as pltpu
from jax.sharding import PartitionSpec as P

NY = 256
CH = 5
ITERS = 2
SLAB_DEV = 4
YB = 32


highest = lax.Precision.HIGHEST


def extended(block, sides, width):
    for axis, dim in sides:
        count = lax.axis_size(axis)
        forward = [(i, i + 1) for i in range(count - 1)]
        backward = [(target, source) for source, target in forward]
        low = lax.ppermute(
            lax.slice_in_dim(block, block.shape[dim] - width, None, axis=dim), axis, forward
        )
        high = lax.ppermute(lax.slice_in_dim(block, 0, width, axis=dim), axis, backward)
        block = jnp.concatenate([low, block, high], axis=dim)
    return block


def shift_pair(low_src, high_src, axis):
    count = lax.axis_size(axis)
    forward = [(i, i + 1) for i in range(count - 1)]
    backward = [(target, source) for source, target in forward]
    low = lax.ppermute(low_src, axis, forward)
    high = lax.ppermute(high_src, axis, backward)
    return low, high


def conv_taps(padded, weights, length):
    running = jnp.einsum("oi,abic->aboc", weights[0], padded[0:length], precision=highest)
    running = running + jnp.einsum(
        "oi,abic->aboc", weights[1], padded[1 : length + 1], precision=highest
    )
    running = running + jnp.einsum(
        "oi,abic->aboc", weights[2], padded[2 : length + 2], precision=highest
    )
    return running


def mix_update(states, hidden, weights):
    return states + jnp.einsum("oh,abhc->aboc", weights, hidden, precision=highest)


def exclusive_slots(labels, count):
    member = (labels[:, None] == jnp.arange(count, dtype=jnp.int32)[None, :]).astype(jnp.int32)
    return jnp.sum((jnp.cumsum(member, axis=0) - member) * member, axis=1)


def primal_kernel(full, hid, rows, nlo, outs, w1_ref, b1_ref, w2_ref, f_ref, *refs):
    if full:
        s_ref, b_ref, lob_ref, hib_ref, o_ref = refs
    else:
        b_ref, lob_ref, hib_ref, o_ref = refs
    nz = b_ref.shape[0]
    yb = b_ref.shape[1]
    nx = b_ref.shape[2]
    nin = CH + 1

    def plane(zz, c, ys):
        if c == CH:
            if zz < 0:
                return lob_ref[zz + nlo, pl.ds(ys, rows), :]
            if zz >= nz:
                return hib_ref[zz - nz, pl.ds(ys, rows), :]
            return b_ref[zz, pl.ds(ys, rows), :]
        return s_ref[zz + 1, c, pl.ds(ys, rows), :]

    chans = list(range(CH + 1)) if full else [CH]
    for slot, z in enumerate(outs):

        def body(i, carry):
            ys = pl.multiple_of(i * rows, rows)
            inputs = [(t, c, plane(z + t - 1, c, ys)) for t in range(3) for c in chans]
            change = [None] * CH
            for h in range(hid):
                acc = None
                for t, c, value in inputs:
                    term = w1_ref[(t * hid + h) * nin + c] * value
                    acc = term if acc is None else acc + term
                acc = jnp.maximum(acc + b1_ref[h], 0.0)
                for c in range(CH):
                    term = w2_ref[c * hid + h] * acc
                    change[c] = term if change[c] is None else change[c] + term
            for c in range(CH):
                if full:
                    out = s_ref[z + 1, c, pl.ds(ys, rows), :] + change[c]
                elif z < 0:
                    out = change[c] * f_ref[0]
                elif z >= nz:
                    out = change[c] * f_ref[1]
                else:
                    out = change[c]
                o_ref[slot, c, pl.ds(ys, rows), :] = out
            return carry

        lax.fori_loop(0, yb // rows, body, 0)


def primal_step(state, back, lo_b, hi_b, flags, w1, b1, w2):
    nz, ny, nx = back.shape
    nlo = lo_b.shape[0]
    hid = b1.shape[0]
    full = state is not None
    if full:
        outs = tuple(range(nz))
        rows = 8
    else:
        outs = tuple(range(-1, nz + 1))
        rows = 16
    smem = pl.BlockSpec(memory_space=pltpu.SMEM)
    spec_s = pl.BlockSpec((nz + 2, CH, YB, nx), lambda j: (0, 0, j, 0))
    spec_b = pl.BlockSpec((nz, YB, nx), lambda j: (0, j, 0))
    spec_h = pl.BlockSpec((nlo, YB, nx), lambda j: (0, j, 0))
    spec_o = pl.BlockSpec((len(outs), CH, YB, nx), lambda j: (0, 0, j, 0))
    operands = (back, lo_b, hi_b)
    specs = [spec_b, spec_h, spec_h]
    if full:
        operands = (state,) + operands
        specs = [spec_s] + specs
    return pl.pallas_call(
        functools.partial(primal_kernel, full, hid, rows, nlo, outs),
        grid=(ny // YB,),
        in_specs=[smem, smem, smem, smem] + specs,
        out_specs=spec_o,
        out_shape=jax.ShapeDtypeStruct((len(outs), CH, ny, nx), jnp.float32),
        compiler_params=pltpu.CompilerParams(dimension_semantics=("arbitrary",)),
    )(w1.reshape(-1), b1, w2.reshape(-1), flags, *operands)


def dual_kernel(full, hid, w1_ref, b1_ref, w2_ref, f_ref, *refs):
    if full:
        s_ref, p_ref, m_ref, o_ref = refs
        outs = range(o_ref.shape[0])
    else:
        m_ref, o_ref = refs
        outs = range(-1, o_ref.shape[0] - 1)
    nv = m_ref.shape[0] - 4
    nin = CH + 2

    def plane(zz, c):
        if c == CH + 1:
            return m_ref[zz + 2]
        if c == CH:
            return p_ref[zz + 1]
        return s_ref[zz + 1, c]

    chans = list(range(CH + 2)) if full else [CH + 1]
    for slot, z in enumerate(outs):
        inputs = [(t, c, plane(z + t - 1, c)) for t in range(3) for c in chans]
        change = [None] * CH
        for h in range(hid):
            acc = None
            for t, c, value in inputs:
                term = w1_ref[(t * hid + h) * nin + c] * value
                acc = term if acc is None else acc + term
            acc = jnp.maximum(acc + b1_ref[h], 0.0)
            for c in range(CH):
                term = w2_ref[c * hid + h] * acc
                change[c] = term if change[c] is None else change[c] + term
        for c in range(CH):
            if full:
                out = s_ref[z + 1, c] + change[c]
            elif z < 0:
                out = change[c] * f_ref[0]
            elif z >= nv:
                out = change[c] * f_ref[1]
            else:
                out = change[c]
            o_ref[slot, c] = out


def dual_step(state, projected, measured_ext, flags, w1, b1, w2):
    nv = measured_ext.shape[0] - 4
    _, rows, cols = measured_ext.shape
    hid = b1.shape[0]
    full = state is not None
    outs = nv if full else nv + 2
    smem = pl.BlockSpec(memory_space=pltpu.SMEM)
    vmem = pl.BlockSpec(memory_space=pltpu.VMEM)
    operands = (state, projected, measured_ext) if full else (measured_ext,)
    return pl.pallas_call(
        functools.partial(dual_kernel, full, hid),
        in_specs=[smem, smem, smem, smem] + [vmem] * len(operands),
        out_specs=vmem,
        out_shape=jax.ShapeDtypeStruct((outs, CH, rows, cols), jnp.float32),
    )(w1.reshape(-1), b1, w2.reshape(-1), flags, *operands)


def local(
    measured,
    bank,
    owner_tile,
    line_index,
    block_index,
    dual_w1,
    dual_b1,
    dual_w2,
    primal_w1,
    primal_b1,
    primal_w2,
):
    view_dev, drow_dev, dcols = measured.shape
    blocks = bank.shape[0]
    width = bank.shape[2]
    per_row = owner_tile.shape[2]
    angle_count = lax.axis_size("angle")
    row_count = lax.axis_size("row")
    owners = angle_count * row_count
    ray_rows = view_dev * drow_dev
    pair_count = ray_rows * per_row
    capacity = 2 * pair_count // owners
    slots = owners * capacity
    lines_dev = SLAB_DEV * NY
    both = ("angle", "row")
    owner_flat = owner_tile.reshape(-1)
    line_flat = line_index.reshape(-1)
    block_flat = block_index.reshape(-1)
    slot_flat = exclusive_slots(owner_flat, owners)
    dest = owner_flat * capacity + slot_flat
    pair_ids = jnp.arange(pair_count, dtype=jnp.int32)
    row_block = (pair_ids // per_row) * blocks + block_flat

    slot_ids = jnp.arange(slots, dtype=jnp.int32)
    hit = dest[None, :] == slot_ids[:, None]
    ids_send = jnp.sum(jnp.where(hit, line_flat[None, :] + 1, 0), axis=1) - 1
    slot_rb = jnp.sum(jnp.where(hit, row_block[None, :] + 1, 0), axis=1) - 1
    gsel = (
        slot_rb[None, :] == jnp.arange(ray_rows * blocks, dtype=jnp.int32)[:, None]
    ).astype(jnp.bfloat16)
    arrived_ids = lax.all_to_all(
        ids_send.reshape(owners, capacity), both, split_axis=0, concat_axis=0, tiled=True
    ).reshape(-1)
    rsel = (
        arrived_ids[:, None] == jnp.arange(lines_dev, dtype=jnp.int32)[None, :]
    ).astype(jnp.bfloat16)
    rsel_t = (
        arrived_ids[None, :] == jnp.arange(lines_dev, dtype=jnp.int32)[:, None]
    ).astype(jnp.bfloat16)
    place = lax.axis_index(both)
    flags = jnp.stack([place > 0, place < owners - 1]).astype(jnp.float32)

    flat_bank = jnp.transpose(bank, (1, 0, 2)).reshape(dcols, blocks * width)
    bank_t = jnp.transpose(bank, (0, 2, 1)).reshape(blocks * width, dcols).astype(jnp.float32)

    def forward(volume_lines):
        chosen = jnp.dot(rsel, volume_lines, preferred_element_type=jnp.float32).astype(
            jnp.bfloat16
        )
        returned = lax.all_to_all(
            chosen.reshape(owners, capacity, width), both, split_axis=0, concat_axis=0, tiled=True
        ).reshape(slots, width)
        summed = jnp.dot(gsel, returned, preferred_element_type=jnp.float32)
        rays = jnp.dot(
            summed.reshape(ray_rows, blocks * width), bank_t, precision=highest
        )
        return rays.reshape(view_dev, drow_dev, dcols)

    def backward(sino_rows):
        all_blocks = jnp.dot(sino_rows, flat_bank, preferred_element_type=jnp.float32).astype(
            jnp.bfloat16
        )
        outgoing = lax.dot_general(
            gsel,
            all_blocks.reshape(ray_rows * blocks, width),
            (((0,), (0,)), ((), ())),
            preferred_element_type=jnp.float32,
        ).astype(jnp.bfloat16)
        arrived = lax.all_to_all(
            outgoing.reshape(owners, capacity, width), both, split_axis=0, concat_axis=0, tiled=True
        ).reshape(slots, width)
        back = jnp.dot(rsel_t, arrived, preferred_element_type=jnp.float32)
        return back.reshape(SLAB_DEV, NY, width)

    angle_place = lax.axis_index("angle")
    view_flags = jnp.stack([angle_place > 0, angle_place < angle_count - 1]).astype(jnp.float32)
    lo_m, hi_m = shift_pair(measured[-2:], measured[:2], "angle")
    measured_ext = jnp.concatenate([lo_m, measured, hi_m], axis=0)
    dual = None
    state = None
    for iteration in range(ITERS):
        if iteration == 0:
            dual = dual_step(
                None, None, measured_ext, view_flags,
                dual_w1[iteration], dual_b1[iteration], dual_w2[iteration],
            )
        else:
            volume_lines = state[1:-1, 1].reshape(lines_dev, width).astype(jnp.bfloat16)
            projected = forward(volume_lines)
            lo_p, hi_p = shift_pair(projected[-1:], projected[:1], "angle")
            projected_ext = jnp.concatenate([lo_p, projected, hi_p], axis=0)
            dual = dual_step(
                dual, projected_ext, measured_ext, view_flags,
                dual_w1[iteration], dual_b1[iteration], dual_w2[iteration],
            )
        core = dual if iteration > 0 else dual[1:-1]
        sino_rows = core[:, 0].reshape(ray_rows, dcols).astype(jnp.bfloat16)
        back = backward(sino_rows)
        if state is None:
            lo_b, hi_b = shift_pair(back[-2:], back[:2], both)
            state = primal_step(
                None, back, lo_b, hi_b, flags,
                primal_w1[iteration], primal_b1[iteration], primal_w2[iteration],
            )
        else:
            lo_b, hi_b = shift_pair(back[-1:], back[:1], both)
            state = primal_step(
                state, back, lo_b, hi_b, flags,
                primal_w1[iteration], primal_b1[iteration], primal_w2[iteration],
            )
    primal_state = jnp.transpose(state, (0, 2, 1, 3))
    dual_state = jnp.transpose(dual, (0, 2, 1, 3))
    return (primal_state, dual_state)


def solution(mesh):
    placed = (
        P("angle", "row", None),
        P(),
        P(("angle", "row"), None, None),
        P(("angle", "row"), None, None),
        P(("angle", "row"), None, None),
        P(),
        P(),
        P(),
        P(),
        P(),
        P(),
    )
    return jax.shard_map(
        local,
        mesh=mesh,
        in_specs=placed,
        out_specs=(P(("angle", "row"), None, None, None), P("angle", "row", None, None)),
        check_vma=False,
    )
```

```python
import functools

import jax
import jax.numpy as jnp
from jax import lax
from jax.experimental import pallas as pl
from jax.experimental.pallas import tpu as pltpu
from jax.sharding import PartitionSpec as P

NY = 256
CH = 5
ITERS = 2
SLAB_DEV = 4
YB = 32


highest = lax.Precision.HIGHEST


def extended(block, sides, width):
    for axis, dim in sides:
        count = lax.axis_size(axis)
        forward = [(i, i + 1) for i in range(count - 1)]
        backward = [(target, source) for source, target in forward]
        low = lax.ppermute(
            lax.slice_in_dim(block, block.shape[dim] - width, None, axis=dim), axis, forward
        )
        high = lax.ppermute(lax.slice_in_dim(block, 0, width, axis=dim), axis, backward)
        block = jnp.concatenate([low, block, high], axis=dim)
    return block


def shift_pair(low_src, high_src, axis):
    count = lax.axis_size(axis)
    forward = [(i, i + 1) for i in range(count - 1)]
    backward = [(target, source) for source, target in forward]
    low = lax.ppermute(low_src, axis, forward)
    high = lax.ppermute(high_src, axis, backward)
    return low, high


def conv_taps(padded, weights, length):
    running = jnp.einsum("oi,abic->aboc", weights[0], padded[0:length], precision=highest)
    running = running + jnp.einsum(
        "oi,abic->aboc", weights[1], padded[1 : length + 1], precision=highest
    )
    running = running + jnp.einsum(
        "oi,abic->aboc", weights[2], padded[2 : length + 2], precision=highest
    )
    return running


def mix_update(states, hidden, weights):
    return states + jnp.einsum("oh,abhc->aboc", weights, hidden, precision=highest)


def exclusive_slots(labels, count):
    member = (labels[:, None] == jnp.arange(count, dtype=jnp.int32)[None, :]).astype(jnp.int32)
    return jnp.sum((jnp.cumsum(member, axis=0) - member) * member, axis=1)


def primal_kernel(full, hid, rows, nlo, outs, wv_ref, f_ref, *refs):
    if full:
        s_ref, b_ref, lob_ref, hib_ref, o_ref = refs
    else:
        b_ref, lob_ref, hib_ref, o_ref = refs
    nz = b_ref.shape[0]
    yb = b_ref.shape[1]
    nx = b_ref.shape[2]
    nin = CH + 1
    bias_at = 3 * hid * nin
    mix_at = bias_at + hid
    halves = [pl.ds(k * 128, 128) for k in range(nx // 128)]

    def plane(zz, c, ys, xs):
        if c == CH:
            if zz < 0:
                return lob_ref[zz + nlo, pl.ds(ys, rows), xs]
            if zz >= nz:
                return hib_ref[zz - nz, pl.ds(ys, rows), xs]
            return b_ref[zz, pl.ds(ys, rows), xs]
        return s_ref[zz + 1, c, pl.ds(ys, rows), xs]

    def weight(idx):
        w = wv_ref[idx]
        if rows == 8:
            return w
        return jnp.concatenate([w] * (rows // 8), axis=0)

    chans = list(range(CH + 1)) if full else [CH]
    for slot, z in enumerate(outs):

        def body(i, carry):
            ys = pl.multiple_of(i * rows, rows)
            inputs = [
                (t, c, [plane(z + t - 1, c, ys, xs) for xs in halves])
                for t in range(3)
                for c in chans
            ]
            change = [[None] * len(halves) for _ in range(CH)]
            for h in range(hid):
                bias = weight(bias_at + h)
                acc = [bias] * len(halves)
                for t, c, values in inputs:
                    w = weight((t * hid + h) * nin + c)
                    acc = [a + w * v for a, v in zip(acc, values)]
                acc = [jnp.maximum(a, 0.0) for a in acc]
                for c in range(CH):
                    w = weight(mix_at + c * hid + h)
                    change[c] = [
                        w * a if old is None else old + w * a for old, a in zip(change[c], acc)
                    ]
            for c in range(CH):
                for k, xs in enumerate(halves):
                    if full:
                        out = s_ref[z + 1, c, pl.ds(ys, rows), xs] + change[c][k]
                    elif z < 0:
                        out = change[c][k] * f_ref[0]
                    elif z >= nz:
                        out = change[c][k] * f_ref[1]
                    else:
                        out = change[c][k]
                    o_ref[slot, c, pl.ds(ys, rows), xs] = out
            return carry

        lax.fori_loop(0, yb // rows, body, 0)


def primal_step(state, back, lo_b, hi_b, flags, w1, b1, w2):
    nz, ny, nx = back.shape
    nlo = lo_b.shape[0]
    hid = b1.shape[0]
    full = state is not None
    if full:
        outs = tuple(range(nz))
        rows = 8
    else:
        outs = tuple(range(-1, nz + 1))
        rows = 16
    packed = jnp.concatenate([w1.reshape(-1), b1, w2.reshape(-1)])
    wv = jnp.broadcast_to(packed[:, None, None], (packed.shape[0], 8, 128))
    smem = pl.BlockSpec(memory_space=pltpu.SMEM)
    spec_w = pl.BlockSpec(wv.shape, lambda j: (0, 0, 0))
    spec_s = pl.BlockSpec((nz + 2, CH, YB, nx), lambda j: (0, 0, j, 0))
    spec_b = pl.BlockSpec((nz, YB, nx), lambda j: (0, j, 0))
    spec_h = pl.BlockSpec((nlo, YB, nx), lambda j: (0, j, 0))
    spec_o = pl.BlockSpec((len(outs), CH, YB, nx), lambda j: (0, 0, j, 0))
    operands = (back, lo_b, hi_b)
    specs = [spec_b, spec_h, spec_h]
    if full:
        operands = (state,) + operands
        specs = [spec_s] + specs
    return pl.pallas_call(
        functools.partial(primal_kernel, full, hid, rows, nlo, outs),
        grid=(ny // YB,),
        in_specs=[spec_w, smem] + specs,
        out_specs=spec_o,
        out_shape=jax.ShapeDtypeStruct((len(outs), CH, ny, nx), jnp.float32),
        compiler_params=pltpu.CompilerParams(dimension_semantics=("arbitrary",)),
    )(wv, flags, *operands)


def dual_kernel(full, hid, w1_ref, b1_ref, w2_ref, f_ref, *refs):
    if full:
        s_ref, p_ref, m_ref, o_ref = refs
        outs = range(o_ref.shape[0])
    else:
        m_ref, o_ref = refs
        outs = range(-1, o_ref.shape[0] - 1)
    nv = m_ref.shape[0] - 4
    nin = CH + 2

    def plane(zz, c):
        if c == CH + 1:
            return m_ref[zz + 2]
        if c == CH:
            return p_ref[zz + 1]
        return s_ref[zz + 1, c]

    chans = list(range(CH + 2)) if full else [CH + 1]
    for slot, z in enumerate(outs):
        inputs = [(t, c, plane(z + t - 1, c)) for t in range(3) for c in chans]
        change = [None] * CH
        for h in range(hid):
            acc = None
            for t, c, value in inputs:
                term = w1_ref[(t * hid + h) * nin + c] * value
                acc = term if acc is None else acc + term
            acc = jnp.maximum(acc + b1_ref[h], 0.0)
            for c in range(CH):
                term = w2_ref[c * hid + h] * acc
                change[c] = term if change[c] is None else change[c] + term
        for c in range(CH):
            if full:
                out = s_ref[z + 1, c] + change[c]
            elif z < 0:
                out = change[c] * f_ref[0]
            elif z >= nv:
                out = change[c] * f_ref[1]
            else:
                out = change[c]
            o_ref[slot, c] = out


def dual_step(state, projected, measured_ext, flags, w1, b1, w2):
    nv = measured_ext.shape[0] - 4
    _, rows, cols = measured_ext.shape
    hid = b1.shape[0]
    full = state is not None
    outs = nv if full else nv + 2
    smem = pl.BlockSpec(memory_space=pltpu.SMEM)
    vmem = pl.BlockSpec(memory_space=pltpu.VMEM)
    operands = (state, projected, measured_ext) if full else (measured_ext,)
    return pl.pallas_call(
        functools.partial(dual_kernel, full, hid),
        in_specs=[smem, smem, smem, smem] + [vmem] * len(operands),
        out_specs=vmem,
        out_shape=jax.ShapeDtypeStruct((outs, CH, rows, cols), jnp.float32),
    )(w1.reshape(-1), b1, w2.reshape(-1), flags, *operands)


def local(
    measured,
    bank,
    owner_tile,
    line_index,
    block_index,
    dual_w1,
    dual_b1,
    dual_w2,
    primal_w1,
    primal_b1,
    primal_w2,
):
    view_dev, drow_dev, dcols = measured.shape
    blocks = bank.shape[0]
    width = bank.shape[2]
    per_row = owner_tile.shape[2]
    angle_count = lax.axis_size("angle")
    row_count = lax.axis_size("row")
    owners = angle_count * row_count
    ray_rows = view_dev * drow_dev
    pair_count = ray_rows * per_row
    capacity = 2 * pair_count // owners
    slots = owners * capacity
    lines_dev = SLAB_DEV * NY
    both = ("angle", "row")
    owner_flat = owner_tile.reshape(-1)
    line_flat = line_index.reshape(-1)
    block_flat = block_index.reshape(-1)
    slot_flat = exclusive_slots(owner_flat, owners)
    dest = owner_flat * capacity + slot_flat
    pair_ids = jnp.arange(pair_count, dtype=jnp.int32)
    row_block = (pair_ids // per_row) * blocks + block_flat

    slot_ids = jnp.arange(slots, dtype=jnp.int32)
    hit = dest[None, :] == slot_ids[:, None]
    ids_send = jnp.sum(jnp.where(hit, line_flat[None, :] + 1, 0), axis=1) - 1
    slot_rb = jnp.sum(jnp.where(hit, row_block[None, :] + 1, 0), axis=1) - 1
    gsel = (
        slot_rb[None, :] == jnp.arange(ray_rows * blocks, dtype=jnp.int32)[:, None]
    ).astype(jnp.bfloat16)
    arrived_ids = lax.all_to_all(
        ids_send.reshape(owners, capacity), both, split_axis=0, concat_axis=0, tiled=True
    ).reshape(-1)
    rsel = (
        arrived_ids[:, None] == jnp.arange(lines_dev, dtype=jnp.int32)[None, :]
    ).astype(jnp.bfloat16)
    rsel_t = (
        arrived_ids[None, :] == jnp.arange(lines_dev, dtype=jnp.int32)[:, None]
    ).astype(jnp.bfloat16)
    place = lax.axis_index(both)
    flags = jnp.stack([place > 0, place < owners - 1]).astype(jnp.float32)

    flat_bank = jnp.transpose(bank, (1, 0, 2)).reshape(dcols, blocks * width)
    bank_t = jnp.transpose(bank, (0, 2, 1)).reshape(blocks * width, dcols).astype(jnp.float32)

    def forward(volume_lines):
        chosen = jnp.dot(rsel, volume_lines, preferred_element_type=jnp.float32).astype(
            jnp.bfloat16
        )
        returned = lax.all_to_all(
            chosen.reshape(owners, capacity, width), both, split_axis=0, concat_axis=0, tiled=True
        ).reshape(slots, width)
        summed = jnp.dot(gsel, returned, preferred_element_type=jnp.float32)
        rays = jnp.dot(
            summed.reshape(ray_rows, blocks * width), bank_t, precision=highest
        )
        return rays.reshape(view_dev, drow_dev, dcols)

    def backward(sino_rows):
        all_blocks = jnp.dot(sino_rows, flat_bank, preferred_element_type=jnp.float32).astype(
            jnp.bfloat16
        )
        outgoing = lax.dot_general(
            gsel,
            all_blocks.reshape(ray_rows * blocks, width),
            (((0,), (0,)), ((), ())),
            preferred_element_type=jnp.float32,
        ).astype(jnp.bfloat16)
        arrived = lax.all_to_all(
            outgoing.reshape(owners, capacity, width), both, split_axis=0, concat_axis=0, tiled=True
        ).reshape(slots, width)
        back = jnp.dot(rsel_t, arrived, preferred_element_type=jnp.float32)
        return back.reshape(SLAB_DEV, NY, width)

    angle_place = lax.axis_index("angle")
    view_flags = jnp.stack([angle_place > 0, angle_place < angle_count - 1]).astype(jnp.float32)
    lo_m, hi_m = shift_pair(measured[-2:], measured[:2], "angle")
    measured_ext = jnp.concatenate([lo_m, measured, hi_m], axis=0)
    dual = None
    state = None
    for iteration in range(ITERS):
        if iteration == 0:
            dual = dual_step(
                None, None, measured_ext, view_flags,
                dual_w1[iteration], dual_b1[iteration], dual_w2[iteration],
            )
        else:
            volume_lines = state[1:-1, 1].reshape(lines_dev, width).astype(jnp.bfloat16)
            projected = forward(volume_lines)
            lo_p, hi_p = shift_pair(projected[-1:], projected[:1], "angle")
            projected_ext = jnp.concatenate([lo_p, projected, hi_p], axis=0)
            dual = dual_step(
                dual, projected_ext, measured_ext, view_flags,
                dual_w1[iteration], dual_b1[iteration], dual_w2[iteration],
            )
        core = dual if iteration > 0 else dual[1:-1]
        sino_rows = core[:, 0].reshape(ray_rows, dcols).astype(jnp.bfloat16)
        back = backward(sino_rows)
        if state is None:
            lo_b, hi_b = shift_pair(back[-2:], back[:2], both)
            state = primal_step(
                None, back, lo_b, hi_b, flags,
                primal_w1[iteration], primal_b1[iteration], primal_w2[iteration],
            )
        else:
            lo_b, hi_b = shift_pair(back[-1:], back[:1], both)
            state = primal_step(
                state, back, lo_b, hi_b, flags,
                primal_w1[iteration], primal_b1[iteration], primal_w2[iteration],
            )
    primal_state = jnp.transpose(state, (0, 2, 1, 3))
    dual_state = jnp.transpose(dual, (0, 2, 1, 3))
    return (primal_state, dual_state)


def solution(mesh):
    placed = (
        P("angle", "row", None),
        P(),
        P(("angle", "row"), None, None),
        P(("angle", "row"), None, None),
        P(("angle", "row"), None, None),
        P(),
        P(),
        P(),
        P(),
        P(),
        P(),
    )
    return jax.shard_map(
        local,
        mesh=mesh,
        in_specs=placed,
        out_specs=(P(("angle", "row"), None, None, None), P("angle", "row", None, None)),
        check_vma=False,
    )
```

```python
import functools

import jax
import jax.numpy as jnp
from jax import lax
from jax.experimental import pallas as pl
from jax.experimental.pallas import tpu as pltpu
from jax.sharding import PartitionSpec as P

NY = 256
CH = 5
ITERS = 2
SLAB_DEV = 4
YB = 32


highest = lax.Precision.HIGHEST


def extended(block, sides, width):
    for axis, dim in sides:
        count = lax.axis_size(axis)
        forward = [(i, i + 1) for i in range(count - 1)]
        backward = [(target, source) for source, target in forward]
        low = lax.ppermute(
            lax.slice_in_dim(block, block.shape[dim] - width, None, axis=dim), axis, forward
        )
        high = lax.ppermute(lax.slice_in_dim(block, 0, width, axis=dim), axis, backward)
        block = jnp.concatenate([low, block, high], axis=dim)
    return block


def shift_pair(low_src, high_src, axis):
    count = lax.axis_size(axis)
    forward = [(i, i + 1) for i in range(count - 1)]
    backward = [(target, source) for source, target in forward]
    low = lax.ppermute(low_src, axis, forward)
    high = lax.ppermute(high_src, axis, backward)
    return low, high


def conv_taps(padded, weights, length):
    running = jnp.einsum("oi,abic->aboc", weights[0], padded[0:length], precision=highest)
    running = running + jnp.einsum(
        "oi,abic->aboc", weights[1], padded[1 : length + 1], precision=highest
    )
    running = running + jnp.einsum(
        "oi,abic->aboc", weights[2], padded[2 : length + 2], precision=highest
    )
    return running


def mix_update(states, hidden, weights):
    return states + jnp.einsum("oh,abhc->aboc", weights, hidden, precision=highest)


def exclusive_slots(labels, count):
    member = (labels[:, None] == jnp.arange(count, dtype=jnp.int32)[None, :]).astype(jnp.int32)
    return jnp.sum((jnp.cumsum(member, axis=0) - member) * member, axis=1)


def primal_kernel(full, hid, rows, nlo, outs, wv_ref, f_ref, *refs):
    if full:
        s_ref, b_ref, lob_ref, hib_ref = refs[:4]
    else:
        b_ref, lob_ref, hib_ref = refs[:3]
    o_ref = refs[-1]
    nz = b_ref.shape[0]
    yb = b_ref.shape[1]
    nx = b_ref.shape[2]
    nin = CH + 1
    bias_at = 3 * hid * nin
    mix_at = bias_at + hid
    halves = [pl.ds(k * 128, 128) for k in range(nx // 128)]
    step = pl.program_id(1)

    def plane(zz, c, ys, xs):
        if c == CH:
            if zz < 0:
                return lob_ref[zz + nlo, pl.ds(ys, rows), xs]
            if zz >= nz:
                return hib_ref[zz - nz, pl.ds(ys, rows), xs]
            return b_ref[zz, pl.ds(ys, rows), xs]
        return s_ref[zz + 1, c, pl.ds(ys, rows), xs]

    def weight(idx):
        w = wv_ref[idx]
        if rows == 8:
            return w
        return jnp.concatenate([w] * (rows // 8), axis=0)

    chans = list(range(CH + 1)) if full else [CH]

    def one_plane(z):
        def body(i, carry):
            ys = pl.multiple_of(i * rows, rows)
            inputs = [
                (t, c, [plane(z + t - 1, c, ys, xs) for xs in halves])
                for t in range(3)
                for c in chans
            ]
            change = [[None] * len(halves) for _ in range(CH)]
            for h in range(hid):
                bias = weight(bias_at + h)
                acc = [bias] * len(halves)
                for t, c, values in inputs:
                    w = weight((t * hid + h) * nin + c)
                    acc = [a + w * v for a, v in zip(acc, values)]
                acc = [jnp.maximum(a, 0.0) for a in acc]
                for c in range(CH):
                    w = weight(mix_at + c * hid + h)
                    change[c] = [
                        w * a if old is None else old + w * a for old, a in zip(change[c], acc)
                    ]
            for c in range(CH):
                for k, xs in enumerate(halves):
                    if full:
                        out = s_ref[z + 1, c, pl.ds(ys, rows), xs] + change[c][k]
                    elif z < 0:
                        out = change[c][k] * f_ref[0]
                    elif z >= nz:
                        out = change[c][k] * f_ref[1]
                    else:
                        out = change[c][k]
                    o_ref[0, c, pl.ds(ys, rows), xs] = out
            return carry

        lax.fori_loop(0, yb // rows, body, 0)

    for idx, z in enumerate(outs):
        pl.when(step == idx)(functools.partial(one_plane, z))


def primal_part(state, back, lo_b, hi_b, flags, wv, hid, outs, slot_of, total, into):
    nz, ny, nx = back.shape
    nlo = lo_b.shape[0]
    full = state is not None
    rows = 8 if full else 16
    smem = pl.BlockSpec(memory_space=pltpu.SMEM)
    spec_w = pl.BlockSpec(wv.shape, lambda j, k: (0, 0, 0))
    spec_s = pl.BlockSpec((nz + 2, CH, YB, nx), lambda j, k: (0, 0, j, 0))
    spec_b = pl.BlockSpec((nz, YB, nx), lambda j, k: (0, j, 0))
    spec_h = pl.BlockSpec((nlo, YB, nx), lambda j, k: (0, j, 0))
    spec_o = pl.BlockSpec((1, CH, YB, nx), lambda j, k: (slot_of(k), 0, j, 0))
    operands = (back, lo_b, hi_b)
    specs = [spec_b, spec_h, spec_h]
    if full:
        operands = (state,) + operands
        specs = [spec_s] + specs
    aliases = {}
    if into is not None:
        aliases = {2 + len(operands): 0}
        operands = operands + (into,)
        specs = specs + [pl.BlockSpec(memory_space=pl.ANY)]
    return pl.pallas_call(
        functools.partial(primal_kernel, full, hid, rows, nlo, outs),
        grid=(ny // YB, len(outs)),
        in_specs=[spec_w, smem] + specs,
        out_specs=spec_o,
        out_shape=jax.ShapeDtypeStruct((total, CH, ny, nx), jnp.float32),
        input_output_aliases=aliases,
        compiler_params=pltpu.CompilerParams(dimension_semantics=("arbitrary", "arbitrary")),
    )(wv, flags, *operands)


def weight_vectors(w1, b1, w2):
    packed = jnp.concatenate([w1.reshape(-1), b1, w2.reshape(-1)])
    return jnp.broadcast_to(packed[:, None, None], (packed.shape[0], 8, 128))


def dual_kernel(full, hid, w1_ref, b1_ref, w2_ref, f_ref, *refs):
    if full:
        s_ref, p_ref, m_ref, o_ref = refs
        outs = range(o_ref.shape[0])
    else:
        m_ref, o_ref = refs
        outs = range(-1, o_ref.shape[0] - 1)
    nv = m_ref.shape[0] - 4
    nin = CH + 2

    def plane(zz, c):
        if c == CH + 1:
            return m_ref[zz + 2]
        if c == CH:
            return p_ref[zz + 1]
        return s_ref[zz + 1, c]

    chans = list(range(CH + 2)) if full else [CH + 1]
    for slot, z in enumerate(outs):
        inputs = [(t, c, plane(z + t - 1, c)) for t in range(3) for c in chans]
        change = [None] * CH
        for h in range(hid):
            acc = None
            for t, c, value in inputs:
                term = w1_ref[(t * hid + h) * nin + c] * value
                acc = term if acc is None else acc + term
            acc = jnp.maximum(acc + b1_ref[h], 0.0)
            for c in range(CH):
                term = w2_ref[c * hid + h] * acc
                change[c] = term if change[c] is None else change[c] + term
        for c in range(CH):
            if full:
                out = s_ref[z + 1, c] + change[c]
            elif z < 0:
                out = change[c] * f_ref[0]
            elif z >= nv:
                out = change[c] * f_ref[1]
            else:
                out = change[c]
            o_ref[slot, c] = out


def dual_step(state, projected, measured_ext, flags, w1, b1, w2):
    nv = measured_ext.shape[0] - 4
    _, rows, cols = measured_ext.shape
    hid = b1.shape[0]
    full = state is not None
    outs = nv if full else nv + 2
    smem = pl.BlockSpec(memory_space=pltpu.SMEM)
    vmem = pl.BlockSpec(memory_space=pltpu.VMEM)
    operands = (state, projected, measured_ext) if full else (measured_ext,)
    return pl.pallas_call(
        functools.partial(dual_kernel, full, hid),
        in_specs=[smem, smem, smem, smem] + [vmem] * len(operands),
        out_specs=vmem,
        out_shape=jax.ShapeDtypeStruct((outs, CH, rows, cols), jnp.float32),
    )(w1.reshape(-1), b1, w2.reshape(-1), flags, *operands)


def local(
    measured,
    bank,
    owner_tile,
    line_index,
    block_index,
    dual_w1,
    dual_b1,
    dual_w2,
    primal_w1,
    primal_b1,
    primal_w2,
):
    view_dev, drow_dev, dcols = measured.shape
    blocks = bank.shape[0]
    width = bank.shape[2]
    per_row = owner_tile.shape[2]
    angle_count = lax.axis_size("angle")
    row_count = lax.axis_size("row")
    owners = angle_count * row_count
    ray_rows = view_dev * drow_dev
    pair_count = ray_rows * per_row
    capacity = 2 * pair_count // owners
    slots = owners * capacity
    lines_dev = SLAB_DEV * NY
    both = ("angle", "row")
    owner_flat = owner_tile.reshape(-1)
    line_flat = line_index.reshape(-1)
    block_flat = block_index.reshape(-1)
    slot_flat = exclusive_slots(owner_flat, owners)
    dest = owner_flat * capacity + slot_flat
    pair_ids = jnp.arange(pair_count, dtype=jnp.int32)
    row_block = (pair_ids // per_row) * blocks + block_flat

    slot_ids = jnp.arange(slots, dtype=jnp.int32)
    hit = dest[None, :] == slot_ids[:, None]
    ids_send = jnp.sum(jnp.where(hit, line_flat[None, :] + 1, 0), axis=1) - 1
    slot_rb = jnp.sum(jnp.where(hit, row_block[None, :] + 1, 0), axis=1) - 1
    gsel = (
        slot_rb[None, :] == jnp.arange(ray_rows * blocks, dtype=jnp.int32)[:, None]
    ).astype(jnp.bfloat16)
    arrived_ids = lax.all_to_all(
        ids_send.reshape(owners, capacity), both, split_axis=0, concat_axis=0, tiled=True
    ).reshape(-1)
    rsel = (
        arrived_ids[:, None] == jnp.arange(lines_dev, dtype=jnp.int32)[None, :]
    ).astype(jnp.bfloat16)
    rsel_t = (
        arrived_ids[None, :] == jnp.arange(lines_dev, dtype=jnp.int32)[:, None]
    ).astype(jnp.bfloat16)
    place = lax.axis_index(both)
    flags = jnp.stack([place > 0, place < owners - 1]).astype(jnp.float32)

    flat_bank = jnp.transpose(bank, (1, 0, 2)).reshape(dcols, blocks * width)
    bank_t = jnp.transpose(bank, (0, 2, 1)).reshape(blocks * width, dcols).astype(jnp.float32)

    def forward(volume_lines):
        chosen = jnp.dot(rsel, volume_lines, preferred_element_type=jnp.float32).astype(
            jnp.bfloat16
        )
        returned = lax.all_to_all(
            chosen.reshape(owners, capacity, width), both, split_axis=0, concat_axis=0, tiled=True
        ).reshape(slots, width)
        summed = jnp.dot(gsel, returned, preferred_element_type=jnp.float32)
        rays = jnp.dot(
            summed.reshape(ray_rows, blocks * width), bank_t, precision=highest
        )
        return rays.reshape(view_dev, drow_dev, dcols)

    def backward(sino_rows):
        all_blocks = jnp.dot(sino_rows, flat_bank, preferred_element_type=jnp.float32).astype(
            jnp.bfloat16
        )
        outgoing = lax.dot_general(
            gsel,
            all_blocks.reshape(ray_rows * blocks, width),
            (((0,), (0,)), ((), ())),
            preferred_element_type=jnp.float32,
        ).astype(jnp.bfloat16)
        arrived = lax.all_to_all(
            outgoing.reshape(owners, capacity, width), both, split_axis=0, concat_axis=0, tiled=True
        ).reshape(slots, width)
        back = jnp.dot(rsel_t, arrived, preferred_element_type=jnp.float32)
        return back.reshape(SLAB_DEV, NY, width)

    angle_place = lax.axis_index("angle")
    view_flags = jnp.stack([angle_place > 0, angle_place < angle_count - 1]).astype(jnp.float32)
    lo_m, hi_m = shift_pair(measured[-2:], measured[:2], "angle")
    measured_ext = jnp.concatenate([lo_m, measured, hi_m], axis=0)
    dual = None
    state = None
    for iteration in range(ITERS):
        if iteration == 0:
            dual = dual_step(
                None, None, measured_ext, view_flags,
                dual_w1[iteration], dual_b1[iteration], dual_w2[iteration],
            )
        else:
            volume_lines = state[1:-1, 1].reshape(lines_dev, width).astype(jnp.bfloat16)
            projected = forward(volume_lines)
            lo_p, hi_p = shift_pair(projected[-1:], projected[:1], "angle")
            projected_ext = jnp.concatenate([lo_p, projected, hi_p], axis=0)
            dual = dual_step(
                dual, projected_ext, measured_ext, view_flags,
                dual_w1[iteration], dual_b1[iteration], dual_w2[iteration],
            )
        core = dual if iteration > 0 else dual[1:-1]
        sino_rows = core[:, 0].reshape(ray_rows, dcols).astype(jnp.bfloat16)
        back = backward(sino_rows)
        wv = weight_vectors(primal_w1[iteration], primal_b1[iteration], primal_w2[iteration])
        hid = primal_b1.shape[1]
        nz = back.shape[0]
        if state is None:
            lo_b, hi_b = shift_pair(back[-2:], back[:2], both)
            inner = primal_part(
                None, back, back[:2], back[:2], flags, wv, hid,
                (1, 2), lambda k: k + 2, nz + 2, None,
            )
            state = primal_part(
                None, back, lo_b, hi_b, flags, wv, hid,
                (-1, 0, nz - 1, nz), lambda k: k + (k // 2) * 2, nz + 2, inner,
            )
        else:
            lo_b, hi_b = shift_pair(back[-1:], back[:1], both)
            inner = primal_part(
                state, back, back[:1], back[:1], flags, wv, hid,
                (1, 2), lambda k: k + 1, nz, None,
            )
            state = primal_part(
                state, back, lo_b, hi_b, flags, wv, hid,
                (0, nz - 1), lambda k: k * 3, nz, inner,
            )
    primal_state = jnp.transpose(state, (0, 2, 1, 3))
    dual_state = jnp.transpose(dual, (0, 2, 1, 3))
    return (primal_state, dual_state)


def solution(mesh):
    placed = (
        P("angle", "row", None),
        P(),
        P(("angle", "row"), None, None),
        P(("angle", "row"), None, None),
        P(("angle", "row"), None, None),
        P(),
        P(),
        P(),
        P(),
        P(),
        P(),
    )
    return jax.shard_map(
        local,
        mesh=mesh,
        in_specs=placed,
        out_specs=(P(("angle", "row"), None, None, None), P("angle", "row", None, None)),
        check_vma=False,
    )
```

```python
import functools

import jax
import jax.numpy as jnp
from jax import lax
from jax.experimental import pallas as pl
from jax.experimental.pallas import tpu as pltpu
from jax.sharding import PartitionSpec as P

NY = 256
CH = 5
ITERS = 2
SLAB_DEV = 4
YB = 128


highest = lax.Precision.HIGHEST


def extended(block, sides, width):
    for axis, dim in sides:
        count = lax.axis_size(axis)
        forward = [(i, i + 1) for i in range(count - 1)]
        backward = [(target, source) for source, target in forward]
        low = lax.ppermute(
            lax.slice_in_dim(block, block.shape[dim] - width, None, axis=dim), axis, forward
        )
        high = lax.ppermute(lax.slice_in_dim(block, 0, width, axis=dim), axis, backward)
        block = jnp.concatenate([low, block, high], axis=dim)
    return block


def shift_pair(low_src, high_src, axis):
    count = lax.axis_size(axis)
    forward = [(i, i + 1) for i in range(count - 1)]
    backward = [(target, source) for source, target in forward]
    low = lax.ppermute(low_src, axis, forward)
    high = lax.ppermute(high_src, axis, backward)
    return low, high


def conv_taps(padded, weights, length):
    running = jnp.einsum("oi,abic->aboc", weights[0], padded[0:length], precision=highest)
    running = running + jnp.einsum(
        "oi,abic->aboc", weights[1], padded[1 : length + 1], precision=highest
    )
    running = running + jnp.einsum(
        "oi,abic->aboc", weights[2], padded[2 : length + 2], precision=highest
    )
    return running


def mix_update(states, hidden, weights):
    return states + jnp.einsum("oh,abhc->aboc", weights, hidden, precision=highest)


def exclusive_slots(labels, count):
    member = (labels[:, None] == jnp.arange(count, dtype=jnp.int32)[None, :]).astype(jnp.int32)
    return jnp.sum((jnp.cumsum(member, axis=0) - member) * member, axis=1)


def primal_kernel(full, hid, rows, nlo, outs, wv_ref, f_ref, *refs):
    if full:
        s_ref, b_ref, lob_ref, hib_ref = refs[:4]
    else:
        b_ref, lob_ref, hib_ref = refs[:3]
    o_ref = refs[-1]
    nz = b_ref.shape[0]
    yb = b_ref.shape[1]
    nx = b_ref.shape[2]
    nin = CH + 1
    bias_at = 3 * hid * nin
    mix_at = bias_at + hid
    halves = [pl.ds(k * 128, 128) for k in range(nx // 128)]
    step = pl.program_id(1)

    def plane(zz, c, ys, xs):
        if c == CH:
            if zz < 0:
                return lob_ref[zz + nlo, pl.ds(ys, rows), xs]
            if zz >= nz:
                return hib_ref[zz - nz, pl.ds(ys, rows), xs]
            return b_ref[zz, pl.ds(ys, rows), xs]
        return s_ref[zz + 1, c, pl.ds(ys, rows), xs]

    def weight(idx):
        w = wv_ref[idx]
        if rows == 8:
            return w
        return jnp.concatenate([w] * (rows // 8), axis=0)

    chans = list(range(CH + 1)) if full else [CH]

    def one_plane(z):
        def body(i, carry):
            ys = pl.multiple_of(i * rows, rows)
            inputs = [
                (t, c, [plane(z + t - 1, c, ys, xs) for xs in halves])
                for t in range(3)
                for c in chans
            ]
            change = [[None] * len(halves) for _ in range(CH)]
            for h in range(hid):
                bias = weight(bias_at + h)
                acc = [bias] * len(halves)
                for t, c, values in inputs:
                    w = weight((t * hid + h) * nin + c)
                    acc = [a + w * v for a, v in zip(acc, values)]
                acc = [jnp.maximum(a, 0.0) for a in acc]
                for c in range(CH):
                    w = weight(mix_at + c * hid + h)
                    change[c] = [
                        w * a if old is None else old + w * a for old, a in zip(change[c], acc)
                    ]
            for c in range(CH):
                for k, xs in enumerate(halves):
                    if full:
                        out = s_ref[z + 1, c, pl.ds(ys, rows), xs] + change[c][k]
                    elif z < 0:
                        out = change[c][k] * f_ref[0]
                    elif z >= nz:
                        out = change[c][k] * f_ref[1]
                    else:
                        out = change[c][k]
                    o_ref[0, c, pl.ds(ys, rows), xs] = out
            return carry

        lax.fori_loop(0, yb // rows, body, 0)

    for idx, z in enumerate(outs):
        pl.when(step == idx)(functools.partial(one_plane, z))


def primal_part(state, back, lo_b, hi_b, flags, wv, hid, outs, slot_of, total, into):
    nz, ny, nx = back.shape
    nlo = lo_b.shape[0]
    full = state is not None
    rows = 8 if full else 16
    smem = pl.BlockSpec(memory_space=pltpu.SMEM)
    spec_w = pl.BlockSpec(wv.shape, lambda j, k: (0, 0, 0))
    spec_s = pl.BlockSpec((nz + 2, CH, YB, nx), lambda j, k: (0, 0, j, 0))
    spec_b = pl.BlockSpec((nz, YB, nx), lambda j, k: (0, j, 0))
    spec_h = pl.BlockSpec((nlo, YB, nx), lambda j, k: (0, j, 0))
    spec_o = pl.BlockSpec((1, CH, YB, nx), lambda j, k: (slot_of(k), 0, j, 0))
    operands = (back, lo_b, hi_b)
    specs = [spec_b, spec_h, spec_h]
    if full:
        operands = (state,) + operands
        specs = [spec_s] + specs
    aliases = {}
    if into is not None:
        aliases = {2 + len(operands): 0}
        operands = operands + (into,)
        specs = specs + [pl.BlockSpec(memory_space=pl.ANY)]
    return pl.pallas_call(
        functools.partial(primal_kernel, full, hid, rows, nlo, outs),
        grid=(ny // YB, len(outs)),
        in_specs=[spec_w, smem] + specs,
        out_specs=spec_o,
        out_shape=jax.ShapeDtypeStruct((total, CH, ny, nx), jnp.float32),
        input_output_aliases=aliases,
        compiler_params=pltpu.CompilerParams(dimension_semantics=("arbitrary", "arbitrary")),
    )(wv, flags, *operands)


def weight_vectors(w1, b1, w2):
    packed = jnp.concatenate([w1.reshape(-1), b1, w2.reshape(-1)])
    return jnp.broadcast_to(packed[:, None, None], (packed.shape[0], 8, 128))


def dual_kernel(full, hid, w1_ref, b1_ref, w2_ref, f_ref, *refs):
    if full:
        s_ref, p_ref, m_ref, o_ref = refs
        outs = range(o_ref.shape[0])
    else:
        m_ref, o_ref = refs
        outs = range(-1, o_ref.shape[0] - 1)
    nv = m_ref.shape[0] - 4
    nin = CH + 2

    def plane(zz, c):
        if c == CH + 1:
            return m_ref[zz + 2]
        if c == CH:
            return p_ref[zz + 1]
        return s_ref[zz + 1, c]

    chans = list(range(CH + 2)) if full else [CH + 1]
    for slot, z in enumerate(outs):
        inputs = [(t, c, plane(z + t - 1, c)) for t in range(3) for c in chans]
        change = [None] * CH
        for h in range(hid):
            acc = None
            for t, c, value in inputs:
                term = w1_ref[(t * hid + h) * nin + c] * value
                acc = term if acc is None else acc + term
            acc = jnp.maximum(acc + b1_ref[h], 0.0)
            for c in range(CH):
                term = w2_ref[c * hid + h] * acc
                change[c] = term if change[c] is None else change[c] + term
        for c in range(CH):
            if full:
                out = s_ref[z + 1, c] + change[c]
            elif z < 0:
                out = change[c] * f_ref[0]
            elif z >= nv:
                out = change[c] * f_ref[1]
            else:
                out = change[c]
            o_ref[slot, c] = out


def dual_step(state, projected, measured_ext, flags, w1, b1, w2):
    nv = measured_ext.shape[0] - 4
    _, rows, cols = measured_ext.shape
    hid = b1.shape[0]
    full = state is not None
    outs = nv if full else nv + 2
    smem = pl.BlockSpec(memory_space=pltpu.SMEM)
    vmem = pl.BlockSpec(memory_space=pltpu.VMEM)
    operands = (state, projected, measured_ext) if full else (measured_ext,)
    return pl.pallas_call(
        functools.partial(dual_kernel, full, hid),
        in_specs=[smem, smem, smem, smem] + [vmem] * len(operands),
        out_specs=vmem,
        out_shape=jax.ShapeDtypeStruct((outs, CH, rows, cols), jnp.float32),
    )(w1.reshape(-1), b1, w2.reshape(-1), flags, *operands)


def local(
    measured,
    bank,
    owner_tile,
    line_index,
    block_index,
    dual_w1,
    dual_b1,
    dual_w2,
    primal_w1,
    primal_b1,
    primal_w2,
):
    view_dev, drow_dev, dcols = measured.shape
    blocks = bank.shape[0]
    width = bank.shape[2]
    per_row = owner_tile.shape[2]
    angle_count = lax.axis_size("angle")
    row_count = lax.axis_size("row")
    owners = angle_count * row_count
    ray_rows = view_dev * drow_dev
    pair_count = ray_rows * per_row
    capacity = 2 * pair_count // owners
    slots = owners * capacity
    lines_dev = SLAB_DEV * NY
    both = ("angle", "row")
    owner_flat = owner_tile.reshape(-1)
    line_flat = line_index.reshape(-1)
    block_flat = block_index.reshape(-1)
    slot_flat = exclusive_slots(owner_flat, owners)
    dest = owner_flat * capacity + slot_flat
    pair_ids = jnp.arange(pair_count, dtype=jnp.int32)
    row_block = (pair_ids // per_row) * blocks + block_flat

    slot_ids = jnp.arange(slots, dtype=jnp.int32)
    hit = dest[None, :] == slot_ids[:, None]
    ids_send = jnp.sum(jnp.where(hit, line_flat[None, :] + 1, 0), axis=1) - 1
    slot_rb = jnp.sum(jnp.where(hit, row_block[None, :] + 1, 0), axis=1) - 1
    gsel = (
        slot_rb[None, :] == jnp.arange(ray_rows * blocks, dtype=jnp.int32)[:, None]
    ).astype(jnp.bfloat16)
    arrived_ids = lax.all_to_all(
        ids_send.reshape(owners, capacity), both, split_axis=0, concat_axis=0, tiled=True
    ).reshape(-1)
    rsel = (
        arrived_ids[:, None] == jnp.arange(lines_dev, dtype=jnp.int32)[None, :]
    ).astype(jnp.bfloat16)
    rsel_t = (
        arrived_ids[None, :] == jnp.arange(lines_dev, dtype=jnp.int32)[:, None]
    ).astype(jnp.bfloat16)
    place = lax.axis_index(both)
    flags = jnp.stack([place > 0, place < owners - 1]).astype(jnp.float32)

    flat_bank = jnp.transpose(bank, (1, 0, 2)).reshape(dcols, blocks * width)
    bank_t = jnp.transpose(bank, (0, 2, 1)).reshape(blocks * width, dcols).astype(jnp.float32)

    def forward(volume_lines):
        chosen = jnp.dot(rsel, volume_lines, preferred_element_type=jnp.float32).astype(
            jnp.bfloat16
        )
        returned = lax.all_to_all(
            chosen.reshape(owners, capacity, width), both, split_axis=0, concat_axis=0, tiled=True
        ).reshape(slots, width)
        summed = jnp.dot(gsel, returned, preferred_element_type=jnp.float32)
        rays = jnp.dot(
            summed.reshape(ray_rows, blocks * width), bank_t, precision=highest
        )
        return rays.reshape(view_dev, drow_dev, dcols)

    def backward(sino_rows):
        all_blocks = jnp.dot(sino_rows, flat_bank, preferred_element_type=jnp.float32).astype(
            jnp.bfloat16
        )
        outgoing = lax.dot_general(
            gsel,
            all_blocks.reshape(ray_rows * blocks, width),
            (((0,), (0,)), ((), ())),
            preferred_element_type=jnp.float32,
        ).astype(jnp.bfloat16)
        arrived = lax.all_to_all(
            outgoing.reshape(owners, capacity, width), both, split_axis=0, concat_axis=0, tiled=True
        ).reshape(slots, width)
        back = jnp.dot(rsel_t, arrived, preferred_element_type=jnp.float32)
        return back.reshape(SLAB_DEV, NY, width)

    angle_place = lax.axis_index("angle")
    view_flags = jnp.stack([angle_place > 0, angle_place < angle_count - 1]).astype(jnp.float32)
    lo_m, hi_m = shift_pair(measured[-2:], measured[:2], "angle")
    measured_ext = jnp.concatenate([lo_m, measured, hi_m], axis=0)
    dual = None
    state = None
    for iteration in range(ITERS):
        if iteration == 0:
            dual = dual_step(
                None, None, measured_ext, view_flags,
                dual_w1[iteration], dual_b1[iteration], dual_w2[iteration],
            )
        else:
            volume_lines = state[1:-1, 1].reshape(lines_dev, width).astype(jnp.bfloat16)
            projected = forward(volume_lines)
            lo_p, hi_p = shift_pair(projected[-1:], projected[:1], "angle")
            projected_ext = jnp.concatenate([lo_p, projected, hi_p], axis=0)
            dual = dual_step(
                dual, projected_ext, measured_ext, view_flags,
                dual_w1[iteration], dual_b1[iteration], dual_w2[iteration],
            )
        core = dual if iteration > 0 else dual[1:-1]
        sino_rows = core[:, 0].reshape(ray_rows, dcols).astype(jnp.bfloat16)
        back = backward(sino_rows)
        wv = weight_vectors(primal_w1[iteration], primal_b1[iteration], primal_w2[iteration])
        hid = primal_b1.shape[1]
        nz = back.shape[0]
        if state is None:
            lo_b, hi_b = shift_pair(back[-2:], back[:2], both)
            inner = primal_part(
                None, back, back[:2], back[:2], flags, wv, hid,
                (1, 2), lambda k: k + 2, nz + 2, None,
            )
            state = primal_part(
                None, back, lo_b, hi_b, flags, wv, hid,
                (-1, 0, nz - 1, nz), lambda k: k + (k // 2) * 2, nz + 2, inner,
            )
        else:
            lo_b, hi_b = shift_pair(back[-1:], back[:1], both)
            inner = primal_part(
                state, back, back[:1], back[:1], flags, wv, hid,
                (1, 2), lambda k: k + 1, nz, None,
            )
            state = primal_part(
                state, back, lo_b, hi_b, flags, wv, hid,
                (0, nz - 1), lambda k: k * 3, nz, inner,
            )
    primal_state = jnp.transpose(state, (0, 2, 1, 3))
    dual_state = jnp.transpose(dual, (0, 2, 1, 3))
    return (primal_state, dual_state)


def solution(mesh):
    placed = (
        P("angle", "row", None),
        P(),
        P(("angle", "row"), None, None),
        P(("angle", "row"), None, None),
        P(("angle", "row"), None, None),
        P(),
        P(),
        P(),
        P(),
        P(),
        P(),
    )
    return jax.shard_map(
        local,
        mesh=mesh,
        in_specs=placed,
        out_specs=(P(("angle", "row"), None, None, None), P("angle", "row", None, None)),
        check_vma=False,
    )
```

```python
import functools

import jax
import jax.numpy as jnp
from jax import lax
from jax.experimental import pallas as pl
from jax.experimental.pallas import tpu as pltpu
from jax.sharding import PartitionSpec as P

NY = 256
CH = 5
ITERS = 2
SLAB_DEV = 4
YB = 128


highest = lax.Precision.HIGHEST


def extended(block, sides, width):
    for axis, dim in sides:
        count = lax.axis_size(axis)
        forward = [(i, i + 1) for i in range(count - 1)]
        backward = [(target, source) for source, target in forward]
        low = lax.ppermute(
            lax.slice_in_dim(block, block.shape[dim] - width, None, axis=dim), axis, forward
        )
        high = lax.ppermute(lax.slice_in_dim(block, 0, width, axis=dim), axis, backward)
        block = jnp.concatenate([low, block, high], axis=dim)
    return block


def shift_pair(low_src, high_src, axis):
    count = lax.axis_size(axis)
    forward = [(i, i + 1) for i in range(count - 1)]
    backward = [(target, source) for source, target in forward]
    low = lax.ppermute(low_src, axis, forward)
    high = lax.ppermute(high_src, axis, backward)
    return low, high


def conv_taps(padded, weights, length):
    running = jnp.einsum("oi,abic->aboc", weights[0], padded[0:length], precision=highest)
    running = running + jnp.einsum(
        "oi,abic->aboc", weights[1], padded[1 : length + 1], precision=highest
    )
    running = running + jnp.einsum(
        "oi,abic->aboc", weights[2], padded[2 : length + 2], precision=highest
    )
    return running


def mix_update(states, hidden, weights):
    return states + jnp.einsum("oh,abhc->aboc", weights, hidden, precision=highest)


def exclusive_slots(labels, count):
    member = (labels[:, None] == jnp.arange(count, dtype=jnp.int32)[None, :]).astype(jnp.int32)
    return jnp.sum((jnp.cumsum(member, axis=0) - member) * member, axis=1)


def primal_kernel(full, hid, rows, nlo, outs, wv_ref, f_ref, *refs):
    if full:
        s_ref, b_ref, lob_ref, hib_ref = refs[:4]
    else:
        b_ref, lob_ref, hib_ref = refs[:3]
    o_ref = refs[-1]
    nz = b_ref.shape[0]
    yb = b_ref.shape[1]
    nx = b_ref.shape[2]
    nin = CH + 1
    bias_at = 3 * hid * nin
    mix_at = bias_at + hid
    halves = [pl.ds(k * 128, 128) for k in range(nx // 128)]
    step = pl.program_id(1)

    def plane(zz, c, ys, xs):
        if c == CH:
            if zz < 0:
                return lob_ref[zz + nlo, pl.ds(ys, rows), xs]
            if zz >= nz:
                return hib_ref[zz - nz, pl.ds(ys, rows), xs]
            return b_ref[zz, pl.ds(ys, rows), xs]
        return s_ref[zz + 1, c, pl.ds(ys, rows), xs]

    def weight(idx):
        w = wv_ref[idx]
        if rows == 8:
            return w
        return jnp.concatenate([w] * (rows // 8), axis=0)

    chans = list(range(CH + 1)) if full else [CH]

    def one_plane(z):
        def body(i, carry):
            ys = pl.multiple_of(i * rows, rows)
            inputs = [
                (t, c, [plane(z + t - 1, c, ys, xs) for xs in halves])
                for t in range(3)
                for c in chans
            ]
            change = [[None] * len(halves) for _ in range(CH)]
            for h in range(hid):
                bias = weight(bias_at + h)
                acc = [bias] * len(halves)
                for t, c, values in inputs:
                    w = weight((t * hid + h) * nin + c)
                    acc = [a + w * v for a, v in zip(acc, values)]
                acc = [jnp.maximum(a, 0.0) for a in acc]
                for c in range(CH):
                    w = weight(mix_at + c * hid + h)
                    change[c] = [
                        w * a if old is None else old + w * a for old, a in zip(change[c], acc)
                    ]
            for c in range(CH):
                for k, xs in enumerate(halves):
                    if full:
                        out = s_ref[z + 1, c, pl.ds(ys, rows), xs] + change[c][k]
                    elif z < 0:
                        out = change[c][k] * f_ref[0]
                    elif z >= nz:
                        out = change[c][k] * f_ref[1]
                    else:
                        out = change[c][k]
                    o_ref[0, c, pl.ds(ys, rows), xs] = out
            return carry

        lax.fori_loop(0, yb // rows, body, 0)

    for idx, z in enumerate(outs):
        pl.when(step == idx)(functools.partial(one_plane, z))


def primal_part(state, back, lo_b, hi_b, flags, wv, hid, outs, slot_of, total, into):
    nz, ny, nx = back.shape
    nlo = lo_b.shape[0]
    full = state is not None
    rows = 8 if full else 16
    smem = pl.BlockSpec(memory_space=pltpu.SMEM)
    spec_w = pl.BlockSpec(wv.shape, lambda j, k: (0, 0, 0))
    spec_s = pl.BlockSpec((nz + 2, CH, YB, nx), lambda j, k: (0, 0, j, 0))
    spec_b = pl.BlockSpec((nz, YB, nx), lambda j, k: (0, j, 0))
    spec_h = pl.BlockSpec((nlo, YB, nx), lambda j, k: (0, j, 0))
    spec_o = pl.BlockSpec((1, CH, YB, nx), lambda j, k: (slot_of(k), 0, j, 0))
    operands = (back, lo_b, hi_b)
    specs = [spec_b, spec_h, spec_h]
    if full:
        operands = (state,) + operands
        specs = [spec_s] + specs
    aliases = {}
    if into is not None:
        aliases = {2 + len(operands): 0}
        operands = operands + (into,)
        specs = specs + [pl.BlockSpec(memory_space=pl.ANY)]
    return pl.pallas_call(
        functools.partial(primal_kernel, full, hid, rows, nlo, outs),
        grid=(ny // YB, len(outs)),
        in_specs=[spec_w, smem] + specs,
        out_specs=spec_o,
        out_shape=jax.ShapeDtypeStruct((total, CH, ny, nx), jnp.float32),
        input_output_aliases=aliases,
        compiler_params=pltpu.CompilerParams(dimension_semantics=("arbitrary", "arbitrary")),
    )(wv, flags, *operands)


def weight_vectors(w1, b1, w2):
    packed = jnp.concatenate([w1.reshape(-1), b1, w2.reshape(-1)])
    return jnp.broadcast_to(packed[:, None, None], (packed.shape[0], 8, 128))


def dual_kernel(full, hid, w1_ref, b1_ref, w2_ref, f_ref, *refs):
    if full:
        s_ref, p_ref, m_ref, o_ref = refs
        outs = range(o_ref.shape[0])
    else:
        m_ref, o_ref = refs
        outs = range(-1, o_ref.shape[0] - 1)
    nv = m_ref.shape[0] - 4
    nin = CH + 2

    def plane(zz, c):
        if c == CH + 1:
            return m_ref[zz + 2]
        if c == CH:
            return p_ref[zz + 1]
        return s_ref[zz + 1, c]

    chans = list(range(CH + 2)) if full else [CH + 1]
    for slot, z in enumerate(outs):
        inputs = [(t, c, plane(z + t - 1, c)) for t in range(3) for c in chans]
        change = [None] * CH
        for h in range(hid):
            acc = None
            for t, c, value in inputs:
                term = w1_ref[(t * hid + h) * nin + c] * value
                acc = term if acc is None else acc + term
            acc = jnp.maximum(acc + b1_ref[h], 0.0)
            for c in range(CH):
                term = w2_ref[c * hid + h] * acc
                change[c] = term if change[c] is None else change[c] + term
        for c in range(CH):
            if full:
                out = s_ref[z + 1, c] + change[c]
            elif z < 0:
                out = change[c] * f_ref[0]
            elif z >= nv:
                out = change[c] * f_ref[1]
            else:
                out = change[c]
            o_ref[slot, c] = out


def dual_step(state, projected, measured_ext, flags, w1, b1, w2):
    nv = measured_ext.shape[0] - 4
    _, rows, cols = measured_ext.shape
    hid = b1.shape[0]
    full = state is not None
    outs = nv if full else nv + 2
    smem = pl.BlockSpec(memory_space=pltpu.SMEM)
    vmem = pl.BlockSpec(memory_space=pltpu.VMEM)
    operands = (state, projected, measured_ext) if full else (measured_ext,)
    return pl.pallas_call(
        functools.partial(dual_kernel, full, hid),
        in_specs=[smem, smem, smem, smem] + [vmem] * len(operands),
        out_specs=vmem,
        out_shape=jax.ShapeDtypeStruct((outs, CH, rows, cols), jnp.float32),
    )(w1.reshape(-1), b1, w2.reshape(-1), flags, *operands)


def local(
    measured,
    bank,
    owner_tile,
    line_index,
    block_index,
    dual_w1,
    dual_b1,
    dual_w2,
    primal_w1,
    primal_b1,
    primal_w2,
):
    view_dev, drow_dev, dcols = measured.shape
    blocks = bank.shape[0]
    width = bank.shape[2]
    per_row = owner_tile.shape[2]
    angle_count = lax.axis_size("angle")
    row_count = lax.axis_size("row")
    owners = angle_count * row_count
    ray_rows = view_dev * drow_dev
    pair_count = ray_rows * per_row
    capacity = 2 * pair_count // owners
    slots = owners * capacity
    lines_dev = SLAB_DEV * NY
    both = ("angle", "row")
    owner_flat = owner_tile.reshape(-1)
    line_flat = line_index.reshape(-1)
    block_flat = block_index.reshape(-1)
    slot_flat = exclusive_slots(owner_flat, owners)
    dest = owner_flat * capacity + slot_flat
    pair_ids = jnp.arange(pair_count, dtype=jnp.int32)
    row_block = (pair_ids // per_row) * blocks + block_flat

    slot_ids = jnp.arange(slots, dtype=jnp.int32)
    hit = dest[None, :] == slot_ids[:, None]
    slot_rb = jnp.sum(jnp.where(hit, row_block[None, :] + 1, 0), axis=1) - 1
    gsel = (
        slot_rb[None, :] == jnp.arange(ray_rows * blocks, dtype=jnp.int32)[:, None]
    ).astype(jnp.bfloat16)
    place = lax.axis_index(both)
    every_line = lax.all_gather(owner_flat * lines_dev + line_flat, both, tiled=True).reshape(
        owners, pair_count
    )
    mine = (every_line // lines_dev) == place
    rank = jnp.cumsum(mine.astype(jnp.int32), axis=1) - 1
    slot_hit = mine[:, None, :] & (rank[:, None, :] == jnp.arange(capacity, dtype=jnp.int32)[None, :, None])
    arrived_ids = (
        jnp.sum(jnp.where(slot_hit, every_line[:, None, :] % lines_dev + 1, 0), axis=2) - 1
    ).reshape(-1)
    rsel = (
        arrived_ids[:, None] == jnp.arange(lines_dev, dtype=jnp.int32)[None, :]
    ).astype(jnp.bfloat16)
    rsel_t = (
        arrived_ids[None, :] == jnp.arange(lines_dev, dtype=jnp.int32)[:, None]
    ).astype(jnp.bfloat16)
    flags = jnp.stack([place > 0, place < owners - 1]).astype(jnp.float32)

    flat_bank = jnp.transpose(bank, (1, 0, 2)).reshape(dcols, blocks * width)
    bank_t = jnp.transpose(bank, (0, 2, 1)).reshape(blocks * width, dcols).astype(jnp.float32)

    def forward(volume_lines):
        chosen = jnp.dot(rsel, volume_lines, preferred_element_type=jnp.float32).astype(
            jnp.bfloat16
        )
        returned = lax.all_to_all(
            chosen.reshape(owners, capacity, width), both, split_axis=0, concat_axis=0, tiled=True
        ).reshape(slots, width)
        summed = jnp.dot(gsel, returned, preferred_element_type=jnp.float32)
        rays = jnp.dot(
            summed.reshape(ray_rows, blocks * width), bank_t, precision=highest
        )
        return rays.reshape(view_dev, drow_dev, dcols)

    def backward(sino_rows):
        all_blocks = jnp.dot(sino_rows, flat_bank, preferred_element_type=jnp.float32).astype(
            jnp.bfloat16
        )
        outgoing = lax.dot_general(
            gsel,
            all_blocks.reshape(ray_rows * blocks, width),
            (((0,), (0,)), ((), ())),
            preferred_element_type=jnp.float32,
        ).astype(jnp.bfloat16)
        arrived = lax.all_to_all(
            outgoing.reshape(owners, capacity, width), both, split_axis=0, concat_axis=0, tiled=True
        ).reshape(slots, width)
        back = jnp.dot(rsel_t, arrived, preferred_element_type=jnp.float32)
        return back.reshape(SLAB_DEV, NY, width)

    angle_place = lax.axis_index("angle")
    view_flags = jnp.stack([angle_place > 0, angle_place < angle_count - 1]).astype(jnp.float32)
    lo_m, hi_m = shift_pair(measured[-2:], measured[:2], "angle")
    measured_ext = jnp.concatenate([lo_m, measured, hi_m], axis=0)
    dual = None
    state = None
    for iteration in range(ITERS):
        if iteration == 0:
            dual = dual_step(
                None, None, measured_ext, view_flags,
                dual_w1[iteration], dual_b1[iteration], dual_w2[iteration],
            )
        else:
            volume_lines = state[1:-1, 1].reshape(lines_dev, width).astype(jnp.bfloat16)
            projected = forward(volume_lines)
            lo_p, hi_p = shift_pair(projected[-1:], projected[:1], "angle")
            projected_ext = jnp.concatenate([lo_p, projected, hi_p], axis=0)
            dual = dual_step(
                dual, projected_ext, measured_ext, view_flags,
                dual_w1[iteration], dual_b1[iteration], dual_w2[iteration],
            )
        core = dual if iteration > 0 else dual[1:-1]
        sino_rows = core[:, 0].reshape(ray_rows, dcols).astype(jnp.bfloat16)
        back = backward(sino_rows)
        wv = weight_vectors(primal_w1[iteration], primal_b1[iteration], primal_w2[iteration])
        hid = primal_b1.shape[1]
        nz = back.shape[0]
        if state is None:
            lo_b, hi_b = shift_pair(back[-2:], back[:2], both)
            inner = primal_part(
                None, back, back[:2], back[:2], flags, wv, hid,
                (1, 2), lambda k: k + 2, nz + 2, None,
            )
            state = primal_part(
                None, back, lo_b, hi_b, flags, wv, hid,
                (-1, 0, nz - 1, nz), lambda k: k + (k // 2) * 2, nz + 2, inner,
            )
        else:
            lo_b, hi_b = shift_pair(back[-1:], back[:1], both)
            inner = primal_part(
                state, back, back[:1], back[:1], flags, wv, hid,
                (1, 2), lambda k: k + 1, nz, None,
            )
            state = primal_part(
                state, back, lo_b, hi_b, flags, wv, hid,
                (0, nz - 1), lambda k: k * 3, nz, inner,
            )
    primal_state = jnp.transpose(state, (0, 2, 1, 3))
    dual_state = jnp.transpose(dual, (0, 2, 1, 3))
    return (primal_state, dual_state)


def solution(mesh):
    placed = (
        P("angle", "row", None),
        P(),
        P(("angle", "row"), None, None),
        P(("angle", "row"), None, None),
        P(("angle", "row"), None, None),
        P(),
        P(),
        P(),
        P(),
        P(),
        P(),
    )
    return jax.shard_map(
        local,
        mesh=mesh,
        in_specs=placed,
        out_specs=(P(("angle", "row"), None, None, None), P("angle", "row", None, None)),
        check_vma=False,
    )
```

```python
import functools

import jax
import jax.numpy as jnp
from jax import lax
from jax.experimental import pallas as pl
from jax.experimental.pallas import tpu as pltpu
from jax.sharding import PartitionSpec as P

NY = 256
CH = 5
ITERS = 2
SLAB_DEV = 4
YB = 128


highest = lax.Precision.HIGHEST


def extended(block, sides, width):
    for axis, dim in sides:
        count = lax.axis_size(axis)
        forward = [(i, i + 1) for i in range(count - 1)]
        backward = [(target, source) for source, target in forward]
        low = lax.ppermute(
            lax.slice_in_dim(block, block.shape[dim] - width, None, axis=dim), axis, forward
        )
        high = lax.ppermute(lax.slice_in_dim(block, 0, width, axis=dim), axis, backward)
        block = jnp.concatenate([low, block, high], axis=dim)
    return block


def shift_pair(low_src, high_src, axis):
    count = lax.axis_size(axis)
    forward = [(i, i + 1) for i in range(count - 1)]
    backward = [(target, source) for source, target in forward]
    low = lax.ppermute(low_src, axis, forward)
    high = lax.ppermute(high_src, axis, backward)
    return low, high


def conv_taps(padded, weights, length):
    running = jnp.einsum("oi,abic->aboc", weights[0], padded[0:length], precision=highest)
    running = running + jnp.einsum(
        "oi,abic->aboc", weights[1], padded[1 : length + 1], precision=highest
    )
    running = running + jnp.einsum(
        "oi,abic->aboc", weights[2], padded[2 : length + 2], precision=highest
    )
    return running


def mix_update(states, hidden, weights):
    return states + jnp.einsum("oh,abhc->aboc", weights, hidden, precision=highest)


def exclusive_slots(labels, count):
    member = (labels[:, None] == jnp.arange(count, dtype=jnp.int32)[None, :]).astype(jnp.int32)
    return jnp.sum((jnp.cumsum(member, axis=0) - member) * member, axis=1)


def primal_kernel(full, hid, rows, nlo, outs, wv_ref, f_ref, *refs):
    if full:
        s_ref, b_ref, lob_ref, hib_ref = refs[:4]
    else:
        b_ref, lob_ref, hib_ref = refs[:3]
    o_ref = refs[-1]
    nz = b_ref.shape[0]
    yb = b_ref.shape[1]
    nx = b_ref.shape[2]
    nin = CH + 1
    bias_at = 3 * hid * nin
    mix_at = bias_at + hid
    halves = [pl.ds(k * 128, 128) for k in range(nx // 128)]
    step = pl.program_id(1)

    def plane(zz, c, ys, xs):
        if c == CH:
            if zz < 0:
                return lob_ref[zz + nlo, pl.ds(ys, rows), xs]
            if zz >= nz:
                return hib_ref[zz - nz, pl.ds(ys, rows), xs]
            return b_ref[zz, pl.ds(ys, rows), xs]
        return s_ref[zz + 1, c, pl.ds(ys, rows), xs]

    def weight(idx):
        w = wv_ref[idx]
        if rows == 8:
            return w
        return jnp.concatenate([w] * (rows // 8), axis=0)

    chans = list(range(CH + 1)) if full else [CH]

    def one_plane(z):
        def body(i, carry):
            ys = pl.multiple_of(i * rows, rows)
            inputs = [
                (t, c, [plane(z + t - 1, c, ys, xs) for xs in halves])
                for t in range(3)
                for c in chans
            ]
            change = [[None] * len(halves) for _ in range(CH)]
            for h in range(hid):
                bias = weight(bias_at + h)
                acc = [bias] * len(halves)
                for t, c, values in inputs:
                    w = weight((t * hid + h) * nin + c)
                    acc = [a + w * v for a, v in zip(acc, values)]
                acc = [jnp.maximum(a, 0.0) for a in acc]
                for c in range(CH):
                    w = weight(mix_at + c * hid + h)
                    change[c] = [
                        w * a if old is None else old + w * a for old, a in zip(change[c], acc)
                    ]
            for c in range(CH):
                for k, xs in enumerate(halves):
                    if full:
                        out = s_ref[z + 1, c, pl.ds(ys, rows), xs] + change[c][k]
                    elif z < 0:
                        out = change[c][k] * f_ref[0]
                    elif z >= nz:
                        out = change[c][k] * f_ref[1]
                    else:
                        out = change[c][k]
                    o_ref[0, c, pl.ds(ys, rows), xs] = out
            return carry

        lax.fori_loop(0, yb // rows, body, 0)

    for idx, z in enumerate(outs):
        pl.when(step == idx)(functools.partial(one_plane, z))


def primal_part(state, back, lo_b, hi_b, flags, wv, hid, outs, slot_of, total, into):
    nz, ny, nx = back.shape
    nlo = lo_b.shape[0]
    full = state is not None
    rows = 8 if full else 16
    smem = pl.BlockSpec(memory_space=pltpu.SMEM)
    spec_w = pl.BlockSpec(wv.shape, lambda j, k: (0, 0, 0))
    spec_s = pl.BlockSpec((nz + 2, CH, YB, nx), lambda j, k: (0, 0, j, 0))
    spec_b = pl.BlockSpec((nz, YB, nx), lambda j, k: (0, j, 0))
    spec_h = pl.BlockSpec((nlo, YB, nx), lambda j, k: (0, j, 0))
    spec_o = pl.BlockSpec((1, CH, YB, nx), lambda j, k: (slot_of(k), 0, j, 0))
    operands = (back, lo_b, hi_b)
    specs = [spec_b, spec_h, spec_h]
    if full:
        operands = (state,) + operands
        specs = [spec_s] + specs
    aliases = {}
    if into is not None:
        aliases = {2 + len(operands): 0}
        operands = operands + (into,)
        specs = specs + [pl.BlockSpec(memory_space=pl.ANY)]
    return pl.pallas_call(
        functools.partial(primal_kernel, full, hid, rows, nlo, outs),
        grid=(ny // YB, len(outs)),
        in_specs=[spec_w, smem] + specs,
        out_specs=spec_o,
        out_shape=jax.ShapeDtypeStruct((total, CH, ny, nx), jnp.float32),
        input_output_aliases=aliases,
        compiler_params=pltpu.CompilerParams(dimension_semantics=("arbitrary", "arbitrary")),
    )(wv, flags, *operands)


def weight_vectors(w1, b1, w2):
    packed = jnp.concatenate([w1.reshape(-1), b1, w2.reshape(-1)])
    return jnp.broadcast_to(packed[:, None, None], (packed.shape[0], 8, 128))


def dual_kernel(full, hid, w1_ref, b1_ref, w2_ref, f_ref, *refs):
    if full:
        s_ref, p_ref, m_ref, o_ref = refs
        outs = range(o_ref.shape[0])
    else:
        m_ref, o_ref = refs
        outs = range(-1, o_ref.shape[0] - 1)
    nv = m_ref.shape[0] - 4
    nin = CH + 2

    def plane(zz, c):
        if c == CH + 1:
            return m_ref[zz + 2]
        if c == CH:
            return p_ref[zz + 1]
        return s_ref[zz + 1, c]

    chans = list(range(CH + 2)) if full else [CH + 1]
    for slot, z in enumerate(outs):
        inputs = [(t, c, plane(z + t - 1, c)) for t in range(3) for c in chans]
        change = [None] * CH
        for h in range(hid):
            acc = None
            for t, c, value in inputs:
                term = w1_ref[(t * hid + h) * nin + c] * value
                acc = term if acc is None else acc + term
            acc = jnp.maximum(acc + b1_ref[h], 0.0)
            for c in range(CH):
                term = w2_ref[c * hid + h] * acc
                change[c] = term if change[c] is None else change[c] + term
        for c in range(CH):
            if full:
                out = s_ref[z + 1, c] + change[c]
            elif z < 0:
                out = change[c] * f_ref[0]
            elif z >= nv:
                out = change[c] * f_ref[1]
            else:
                out = change[c]
            o_ref[slot, c] = out


def dual_step(state, projected, measured_ext, flags, w1, b1, w2):
    nv = measured_ext.shape[0] - 4
    _, rows, cols = measured_ext.shape
    hid = b1.shape[0]
    full = state is not None
    outs = nv if full else nv + 2
    smem = pl.BlockSpec(memory_space=pltpu.SMEM)
    vmem = pl.BlockSpec(memory_space=pltpu.VMEM)
    operands = (state, projected, measured_ext) if full else (measured_ext,)
    return pl.pallas_call(
        functools.partial(dual_kernel, full, hid),
        in_specs=[smem, smem, smem, smem] + [vmem] * len(operands),
        out_specs=vmem,
        out_shape=jax.ShapeDtypeStruct((outs, CH, rows, cols), jnp.float32),
    )(w1.reshape(-1), b1, w2.reshape(-1), flags, *operands)


def local(
    measured,
    bank,
    owner_tile,
    line_index,
    block_index,
    dual_w1,
    dual_b1,
    dual_w2,
    primal_w1,
    primal_b1,
    primal_w2,
):
    view_dev, drow_dev, dcols = measured.shape
    blocks = bank.shape[0]
    width = bank.shape[2]
    per_row = owner_tile.shape[2]
    angle_count = lax.axis_size("angle")
    row_count = lax.axis_size("row")
    owners = angle_count * row_count
    ray_rows = view_dev * drow_dev
    pair_count = ray_rows * per_row
    capacity = 2 * pair_count // owners
    slots = owners * capacity
    lines_dev = SLAB_DEV * NY
    both = ("angle", "row")
    owner_flat = owner_tile.reshape(-1)
    line_flat = line_index.reshape(-1)
    block_flat = block_index.reshape(-1)
    slot_flat = exclusive_slots(owner_flat, owners)
    dest = owner_flat * capacity + slot_flat
    pair_ids = jnp.arange(pair_count, dtype=jnp.int32)
    row_block = (pair_ids // per_row) * blocks + block_flat

    slot_ids = jnp.arange(slots, dtype=jnp.int32)
    hit = dest[None, :] == slot_ids[:, None]
    ids_send = jnp.sum(jnp.where(hit, line_flat[None, :] + 1, 0), axis=1) - 1
    slot_rb = jnp.sum(jnp.where(hit, row_block[None, :] + 1, 0), axis=1) - 1
    gsel = (
        slot_rb[None, :] == jnp.arange(ray_rows * blocks, dtype=jnp.int32)[:, None]
    ).astype(jnp.bfloat16)
    coded = (ids_send + 1).reshape(owners, capacity)
    code_row = jnp.concatenate(
        [coded // 32, coded % 32, jnp.zeros((owners, width - 2 * capacity), jnp.int32)], axis=1
    ).astype(jnp.bfloat16)[:, None, :]
    selectors = {}

    def line_selectors(arrived_codes):
        codes = arrived_codes.astype(jnp.int32)
        arrived_ids = (codes[:, :capacity] * 32 + codes[:, capacity : 2 * capacity] - 1).reshape(-1)
        selectors["rsel"] = (
            arrived_ids[:, None] == jnp.arange(lines_dev, dtype=jnp.int32)[None, :]
        ).astype(jnp.bfloat16)
        selectors["rsel_t"] = (
            arrived_ids[None, :] == jnp.arange(lines_dev, dtype=jnp.int32)[:, None]
        ).astype(jnp.bfloat16)
    place = lax.axis_index(both)
    flags = jnp.stack([place > 0, place < owners - 1]).astype(jnp.float32)

    flat_bank = jnp.transpose(bank, (1, 0, 2)).reshape(dcols, blocks * width)
    bank_t = jnp.transpose(bank, (0, 2, 1)).reshape(blocks * width, dcols).astype(jnp.float32)

    def forward(volume_lines):
        chosen = jnp.dot(selectors["rsel"], volume_lines, preferred_element_type=jnp.float32).astype(
            jnp.bfloat16
        )
        returned = lax.all_to_all(
            chosen.reshape(owners, capacity, width), both, split_axis=0, concat_axis=0, tiled=True
        ).reshape(slots, width)
        summed = jnp.dot(gsel, returned, preferred_element_type=jnp.float32)
        rays = jnp.dot(
            summed.reshape(ray_rows, blocks * width), bank_t, precision=highest
        )
        return rays.reshape(view_dev, drow_dev, dcols)

    def backward(sino_rows):
        all_blocks = jnp.dot(sino_rows, flat_bank, preferred_element_type=jnp.float32).astype(
            jnp.bfloat16
        )
        outgoing = lax.dot_general(
            gsel,
            all_blocks.reshape(ray_rows * blocks, width),
            (((0,), (0,)), ((), ())),
            preferred_element_type=jnp.float32,
        ).astype(jnp.bfloat16)
        outgoing = outgoing.reshape(owners, capacity, width)
        if not selectors:
            outgoing = jnp.concatenate([outgoing, code_row], axis=1)
        arrived = lax.all_to_all(outgoing, both, split_axis=0, concat_axis=0, tiled=True)
        if not selectors:
            line_selectors(arrived[:, capacity, :])
            arrived = arrived[:, :capacity]
        arrived = arrived.reshape(slots, width)
        back = jnp.dot(selectors["rsel_t"], arrived, preferred_element_type=jnp.float32)
        return back.reshape(SLAB_DEV, NY, width)

    angle_place = lax.axis_index("angle")
    view_flags = jnp.stack([angle_place > 0, angle_place < angle_count - 1]).astype(jnp.float32)
    lo_m, hi_m = shift_pair(measured[-2:], measured[:2], "angle")
    measured_ext = jnp.concatenate([lo_m, measured, hi_m], axis=0)
    dual = None
    state = None
    for iteration in range(ITERS):
        if iteration == 0:
            dual = dual_step(
                None, None, measured_ext, view_flags,
                dual_w1[iteration], dual_b1[iteration], dual_w2[iteration],
            )
        else:
            volume_lines = state[1:-1, 1].reshape(lines_dev, width).astype(jnp.bfloat16)
            projected = forward(volume_lines)
            lo_p, hi_p = shift_pair(projected[-1:], projected[:1], "angle")
            projected_ext = jnp.concatenate([lo_p, projected, hi_p], axis=0)
            dual = dual_step(
                dual, projected_ext, measured_ext, view_flags,
                dual_w1[iteration], dual_b1[iteration], dual_w2[iteration],
            )
        core = dual if iteration > 0 else dual[1:-1]
        sino_rows = core[:, 0].reshape(ray_rows, dcols).astype(jnp.bfloat16)
        back = backward(sino_rows)
        wv = weight_vectors(primal_w1[iteration], primal_b1[iteration], primal_w2[iteration])
        hid = primal_b1.shape[1]
        nz = back.shape[0]
        if state is None:
            lo_b, hi_b = shift_pair(back[-2:], back[:2], both)
            inner = primal_part(
                None, back, back[:2], back[:2], flags, wv, hid,
                (1, 2), lambda k: k + 2, nz + 2, None,
            )
            state = primal_part(
                None, back, lo_b, hi_b, flags, wv, hid,
                (-1, 0, nz - 1, nz), lambda k: k + (k // 2) * 2, nz + 2, inner,
            )
        else:
            lo_b, hi_b = shift_pair(back[-1:], back[:1], both)
            inner = primal_part(
                state, back, back[:1], back[:1], flags, wv, hid,
                (1, 2), lambda k: k + 1, nz, None,
            )
            state = primal_part(
                state, back, lo_b, hi_b, flags, wv, hid,
                (0, nz - 1), lambda k: k * 3, nz, inner,
            )
    primal_state = jnp.transpose(state, (0, 2, 1, 3))
    dual_state = jnp.transpose(dual, (0, 2, 1, 3))
    return (primal_state, dual_state)


def solution(mesh):
    placed = (
        P("angle", "row", None),
        P(),
        P(("angle", "row"), None, None),
        P(("angle", "row"), None, None),
        P(("angle", "row"), None, None),
        P(),
        P(),
        P(),
        P(),
        P(),
        P(),
    )
    return jax.shard_map(
        local,
        mesh=mesh,
        in_specs=placed,
        out_specs=(P(("angle", "row"), None, None, None), P("angle", "row", None, None)),
        check_vma=False,
    )
```

```python
import functools

import jax
import jax.numpy as jnp
from jax import lax
from jax.experimental import pallas as pl
from jax.experimental.pallas import tpu as pltpu
from jax.sharding import PartitionSpec as P

NY = 256
CH = 5
ITERS = 2
SLAB_DEV = 4
YB = 128


highest = lax.Precision.HIGHEST


def extended(block, sides, width):
    for axis, dim in sides:
        count = lax.axis_size(axis)
        forward = [(i, i + 1) for i in range(count - 1)]
        backward = [(target, source) for source, target in forward]
        low = lax.ppermute(
            lax.slice_in_dim(block, block.shape[dim] - width, None, axis=dim), axis, forward
        )
        high = lax.ppermute(lax.slice_in_dim(block, 0, width, axis=dim), axis, backward)
        block = jnp.concatenate([low, block, high], axis=dim)
    return block


def shift_pair(low_src, high_src, axis):
    count = lax.axis_size(axis)
    forward = [(i, i + 1) for i in range(count - 1)]
    backward = [(target, source) for source, target in forward]
    low = lax.ppermute(low_src, axis, forward)
    high = lax.ppermute(high_src, axis, backward)
    return low, high


def conv_taps(padded, weights, length):
    running = jnp.einsum("oi,abic->aboc", weights[0], padded[0:length], precision=highest)
    running = running + jnp.einsum(
        "oi,abic->aboc", weights[1], padded[1 : length + 1], precision=highest
    )
    running = running + jnp.einsum(
        "oi,abic->aboc", weights[2], padded[2 : length + 2], precision=highest
    )
    return running


def mix_update(states, hidden, weights):
    return states + jnp.einsum("oh,abhc->aboc", weights, hidden, precision=highest)


def exclusive_slots(labels, count):
    member = (labels[:, None] == jnp.arange(count, dtype=jnp.int32)[None, :]).astype(jnp.int32)
    return jnp.sum((jnp.cumsum(member, axis=0) - member) * member, axis=1)


def primal_kernel(full, hid, rows, nlo, outs, wv_ref, f_ref, *refs):
    if full:
        s_ref, b_ref, lob_ref, hib_ref = refs[:4]
    else:
        b_ref, lob_ref, hib_ref = refs[:3]
    o_ref = refs[-1]
    nz = b_ref.shape[0]
    yb = b_ref.shape[1]
    nx = b_ref.shape[2]
    nin = CH + 1
    bias_at = 3 * hid * nin
    mix_at = bias_at + hid
    halves = [(r, pl.ds(k * 128, 128)) for r in range(0, rows, 8) for k in range(nx // 128)]
    step = pl.program_id(1)

    def plane(zz, c, ys, xs):
        if c == CH:
            if zz < 0:
                return lob_ref[zz + nlo, pl.ds(ys, 8), xs]
            if zz >= nz:
                return hib_ref[zz - nz, pl.ds(ys, 8), xs]
            return b_ref[zz, pl.ds(ys, 8), xs]
        return s_ref[zz + 1, c, pl.ds(ys, 8), xs]

    def weight(idx):
        return wv_ref[idx]

    chans = list(range(CH + 1)) if full else [CH]

    def one_plane(z):
        def body(i, carry):
            ys = pl.multiple_of(i * rows, rows)
            taps = [(t, c) for t in range(3) for c in chans]
            change = [[None] * len(halves) for _ in range(CH)]
            group = 4 if full else hid
            for first in range(0, hid, group):
                members = range(first, first + group)
                acc = {h: [weight(bias_at + h)] * len(halves) for h in members}
                for t, c in taps:
                    values = [plane(z + t - 1, c, ys + r, xs) for r, xs in halves]
                    for h in members:
                        w = weight((t * hid + h) * nin + c)
                        acc[h] = [a + w * v for a, v in zip(acc[h], values)]
                for h in members:
                    hidden = [jnp.maximum(a, 0.0) for a in acc[h]]
                    for c in range(CH):
                        w = weight(mix_at + c * hid + h)
                        change[c] = [
                            w * a if old is None else old + w * a
                            for old, a in zip(change[c], hidden)
                        ]
            for c in range(CH):
                for k, (r, xs) in enumerate(halves):
                    if full:
                        out = s_ref[z + 1, c, pl.ds(ys + r, 8), xs] + change[c][k]
                    elif z < 0:
                        out = change[c][k] * f_ref[0]
                    elif z >= nz:
                        out = change[c][k] * f_ref[1]
                    else:
                        out = change[c][k]
                    o_ref[0, c, pl.ds(ys + r, 8), xs] = out
            return carry

        lax.fori_loop(0, yb // rows, body, 0)

    for idx, z in enumerate(outs):
        pl.when(step == idx)(functools.partial(one_plane, z))


def primal_part(state, back, lo_b, hi_b, flags, wv, hid, outs, slot_of, total, into):
    nz, ny, nx = back.shape
    nlo = lo_b.shape[0]
    full = state is not None
    rows = 16
    smem = pl.BlockSpec(memory_space=pltpu.SMEM)
    spec_w = pl.BlockSpec(wv.shape, lambda j, k: (0, 0, 0))
    spec_s = pl.BlockSpec((nz + 2, CH, YB, nx), lambda j, k: (0, 0, j, 0))
    spec_b = pl.BlockSpec((nz, YB, nx), lambda j, k: (0, j, 0))
    spec_h = pl.BlockSpec((nlo, YB, nx), lambda j, k: (0, j, 0))
    spec_o = pl.BlockSpec((1, CH, YB, nx), lambda j, k: (slot_of(k), 0, j, 0))
    operands = (back, lo_b, hi_b)
    specs = [spec_b, spec_h, spec_h]
    if full:
        operands = (state,) + operands
        specs = [spec_s] + specs
    aliases = {}
    if into is not None:
        aliases = {2 + len(operands): 0}
        operands = operands + (into,)
        specs = specs + [pl.BlockSpec(memory_space=pl.ANY)]
    return pl.pallas_call(
        functools.partial(primal_kernel, full, hid, rows, nlo, outs),
        grid=(ny // YB, len(outs)),
        in_specs=[spec_w, smem] + specs,
        out_specs=spec_o,
        out_shape=jax.ShapeDtypeStruct((total, CH, ny, nx), jnp.float32),
        input_output_aliases=aliases,
        compiler_params=pltpu.CompilerParams(dimension_semantics=("arbitrary", "arbitrary")),
    )(wv, flags, *operands)


def weight_vectors(w1, b1, w2):
    packed = jnp.concatenate([w1.reshape(-1), b1, w2.reshape(-1)])
    return jnp.broadcast_to(packed[:, None, None], (packed.shape[0], 8, 128))


def dual_kernel(full, hid, w1_ref, b1_ref, w2_ref, f_ref, *refs):
    if full:
        s_ref, p_ref, m_ref, o_ref = refs
        outs = range(o_ref.shape[0])
    else:
        m_ref, o_ref = refs
        outs = range(-1, o_ref.shape[0] - 1)
    nv = m_ref.shape[0] - 4
    nin = CH + 2

    def plane(zz, c):
        if c == CH + 1:
            return m_ref[zz + 2]
        if c == CH:
            return p_ref[zz + 1]
        return s_ref[zz + 1, c]

    chans = list(range(CH + 2)) if full else [CH + 1]
    for slot, z in enumerate(outs):
        inputs = [(t, c, plane(z + t - 1, c)) for t in range(3) for c in chans]
        change = [None] * CH
        for h in range(hid):
            acc = None
            for t, c, value in inputs:
                term = w1_ref[(t * hid + h) * nin + c] * value
                acc = term if acc is None else acc + term
            acc = jnp.maximum(acc + b1_ref[h], 0.0)
            for c in range(CH):
                term = w2_ref[c * hid + h] * acc
                change[c] = term if change[c] is None else change[c] + term
        for c in range(CH):
            if full:
                out = s_ref[z + 1, c] + change[c]
            elif z < 0:
                out = change[c] * f_ref[0]
            elif z >= nv:
                out = change[c] * f_ref[1]
            else:
                out = change[c]
            o_ref[slot, c] = out


def dual_step(state, projected, measured_ext, flags, w1, b1, w2):
    nv = measured_ext.shape[0] - 4
    _, rows, cols = measured_ext.shape
    hid = b1.shape[0]
    full = state is not None
    outs = nv if full else nv + 2
    smem = pl.BlockSpec(memory_space=pltpu.SMEM)
    vmem = pl.BlockSpec(memory_space=pltpu.VMEM)
    operands = (state, projected, measured_ext) if full else (measured_ext,)
    return pl.pallas_call(
        functools.partial(dual_kernel, full, hid),
        in_specs=[smem, smem, smem, smem] + [vmem] * len(operands),
        out_specs=vmem,
        out_shape=jax.ShapeDtypeStruct((outs, CH, rows, cols), jnp.float32),
    )(w1.reshape(-1), b1, w2.reshape(-1), flags, *operands)


def local(
    measured,
    bank,
    owner_tile,
    line_index,
    block_index,
    dual_w1,
    dual_b1,
    dual_w2,
    primal_w1,
    primal_b1,
    primal_w2,
):
    view_dev, drow_dev, dcols = measured.shape
    blocks = bank.shape[0]
    width = bank.shape[2]
    per_row = owner_tile.shape[2]
    angle_count = lax.axis_size("angle")
    row_count = lax.axis_size("row")
    owners = angle_count * row_count
    ray_rows = view_dev * drow_dev
    pair_count = ray_rows * per_row
    capacity = 2 * pair_count // owners
    slots = owners * capacity
    lines_dev = SLAB_DEV * NY
    both = ("angle", "row")
    owner_flat = owner_tile.reshape(-1)
    line_flat = line_index.reshape(-1)
    block_flat = block_index.reshape(-1)
    slot_flat = exclusive_slots(owner_flat, owners)
    dest = owner_flat * capacity + slot_flat
    pair_ids = jnp.arange(pair_count, dtype=jnp.int32)
    row_block = (pair_ids // per_row) * blocks + block_flat

    slot_ids = jnp.arange(slots, dtype=jnp.int32)
    hit = dest[None, :] == slot_ids[:, None]
    ids_send = jnp.sum(jnp.where(hit, line_flat[None, :] + 1, 0), axis=1) - 1
    slot_rb = jnp.sum(jnp.where(hit, row_block[None, :] + 1, 0), axis=1) - 1
    gsel = (
        slot_rb[None, :] == jnp.arange(ray_rows * blocks, dtype=jnp.int32)[:, None]
    ).astype(jnp.bfloat16)
    coded = (ids_send + 1).reshape(owners, capacity)
    code_row = jnp.concatenate(
        [coded // 32, coded % 32, jnp.zeros((owners, width - 2 * capacity), jnp.int32)], axis=1
    ).astype(jnp.bfloat16)[:, None, :]
    selectors = {}

    def line_selectors(arrived_codes):
        codes = arrived_codes.astype(jnp.int32)
        arrived_ids = (codes[:, :capacity] * 32 + codes[:, capacity : 2 * capacity] - 1).reshape(-1)
        selectors["rsel"] = (
            arrived_ids[:, None] == jnp.arange(lines_dev, dtype=jnp.int32)[None, :]
        ).astype(jnp.bfloat16)
        selectors["rsel_t"] = (
            arrived_ids[None, :] == jnp.arange(lines_dev, dtype=jnp.int32)[:, None]
        ).astype(jnp.bfloat16)
    place = lax.axis_index(both)
    flags = jnp.stack([place > 0, place < owners - 1]).astype(jnp.float32)

    flat_bank = jnp.transpose(bank, (1, 0, 2)).reshape(dcols, blocks * width)
    bank_t = jnp.transpose(bank, (0, 2, 1)).reshape(blocks * width, dcols).astype(jnp.float32)

    def forward(volume_lines):
        chosen = jnp.dot(selectors["rsel"], volume_lines, preferred_element_type=jnp.float32).astype(
            jnp.bfloat16
        )
        returned = lax.all_to_all(
            chosen.reshape(owners, capacity, width), both, split_axis=0, concat_axis=0, tiled=True
        ).reshape(slots, width)
        summed = jnp.dot(gsel, returned, preferred_element_type=jnp.float32)
        rays = jnp.dot(
            summed.reshape(ray_rows, blocks * width), bank_t, precision=highest
        )
        return rays.reshape(view_dev, drow_dev, dcols)

    def backward(sino_rows):
        all_blocks = jnp.dot(sino_rows, flat_bank, preferred_element_type=jnp.float32).astype(
            jnp.bfloat16
        )
        outgoing = lax.dot_general(
            gsel,
            all_blocks.reshape(ray_rows * blocks, width),
            (((0,), (0,)), ((), ())),
            preferred_element_type=jnp.float32,
        ).astype(jnp.bfloat16)
        outgoing = outgoing.reshape(owners, capacity, width)
        if not selectors:
            outgoing = jnp.concatenate([outgoing, code_row], axis=1)
        arrived = lax.all_to_all(outgoing, both, split_axis=0, concat_axis=0, tiled=True)
        if not selectors:
            line_selectors(arrived[:, capacity, :])
            arrived = arrived[:, :capacity]
        arrived = arrived.reshape(slots, width)
        back = jnp.dot(selectors["rsel_t"], arrived, preferred_element_type=jnp.float32)
        return back.reshape(SLAB_DEV, NY, width)

    angle_place = lax.axis_index("angle")
    view_flags = jnp.stack([angle_place > 0, angle_place < angle_count - 1]).astype(jnp.float32)
    lo_m, hi_m = shift_pair(measured[-2:], measured[:2], "angle")
    measured_ext = jnp.concatenate([lo_m, measured, hi_m], axis=0)
    dual = None
    state = None
    for iteration in range(ITERS):
        if iteration == 0:
            dual = dual_step(
                None, None, measured_ext, view_flags,
                dual_w1[iteration], dual_b1[iteration], dual_w2[iteration],
            )
        else:
            volume_lines = state[1:-1, 1].reshape(lines_dev, width).astype(jnp.bfloat16)
            projected = forward(volume_lines)
            lo_p, hi_p = shift_pair(projected[-1:], projected[:1], "angle")
            projected_ext = jnp.concatenate([lo_p, projected, hi_p], axis=0)
            dual = dual_step(
                dual, projected_ext, measured_ext, view_flags,
                dual_w1[iteration], dual_b1[iteration], dual_w2[iteration],
            )
        core = dual if iteration > 0 else dual[1:-1]
        sino_rows = core[:, 0].reshape(ray_rows, dcols).astype(jnp.bfloat16)
        back = backward(sino_rows)
        wv = weight_vectors(primal_w1[iteration], primal_b1[iteration], primal_w2[iteration])
        hid = primal_b1.shape[1]
        nz = back.shape[0]
        if state is None:
            lo_b, hi_b = shift_pair(back[-2:], back[:2], both)
            inner = primal_part(
                None, back, back[:2], back[:2], flags, wv, hid,
                (1, 2), lambda k: k + 2, nz + 2, None,
            )
            state = primal_part(
                None, back, lo_b, hi_b, flags, wv, hid,
                (-1, 0, nz - 1, nz), lambda k: k + (k // 2) * 2, nz + 2, inner,
            )
        else:
            lo_b, hi_b = shift_pair(back[-1:], back[:1], both)
            inner = primal_part(
                state, back, back[:1], back[:1], flags, wv, hid,
                (1, 2), lambda k: k + 1, nz, None,
            )
            state = primal_part(
                state, back, lo_b, hi_b, flags, wv, hid,
                (0, nz - 1), lambda k: k * 3, nz, inner,
            )
    primal_state = jnp.transpose(state, (0, 2, 1, 3))
    dual_state = jnp.transpose(dual, (0, 2, 1, 3))
    return (primal_state, dual_state)


def solution(mesh):
    placed = (
        P("angle", "row", None),
        P(),
        P(("angle", "row"), None, None),
        P(("angle", "row"), None, None),
        P(("angle", "row"), None, None),
        P(),
        P(),
        P(),
        P(),
        P(),
        P(),
    )
    return jax.shard_map(
        local,
        mesh=mesh,
        in_specs=placed,
        out_specs=(P(("angle", "row"), None, None, None), P("angle", "row", None, None)),
        check_vma=False,
    )
```

```python
import functools

import jax
import jax.numpy as jnp
from jax import lax
from jax.experimental import pallas as pl
from jax.experimental.pallas import tpu as pltpu
from jax.sharding import PartitionSpec as P

NY = 256
CH = 5
ITERS = 2
SLAB_DEV = 4
YB = 128


highest = lax.Precision.HIGHEST


def extended(block, sides, width):
    for axis, dim in sides:
        count = lax.axis_size(axis)
        forward = [(i, i + 1) for i in range(count - 1)]
        backward = [(target, source) for source, target in forward]
        low = lax.ppermute(
            lax.slice_in_dim(block, block.shape[dim] - width, None, axis=dim), axis, forward
        )
        high = lax.ppermute(lax.slice_in_dim(block, 0, width, axis=dim), axis, backward)
        block = jnp.concatenate([low, block, high], axis=dim)
    return block


def shift_pair(low_src, high_src, axis):
    count = lax.axis_size(axis)
    forward = [(i, i + 1) for i in range(count - 1)]
    backward = [(target, source) for source, target in forward]
    low = lax.ppermute(low_src, axis, forward)
    high = lax.ppermute(high_src, axis, backward)
    return low, high


def conv_taps(padded, weights, length):
    running = jnp.einsum("oi,abic->aboc", weights[0], padded[0:length], precision=highest)
    running = running + jnp.einsum(
        "oi,abic->aboc", weights[1], padded[1 : length + 1], precision=highest
    )
    running = running + jnp.einsum(
        "oi,abic->aboc", weights[2], padded[2 : length + 2], precision=highest
    )
    return running


def mix_update(states, hidden, weights):
    return states + jnp.einsum("oh,abhc->aboc", weights, hidden, precision=highest)


def exclusive_slots(labels, count):
    member = (labels[:, None] == jnp.arange(count, dtype=jnp.int32)[None, :]).astype(jnp.int32)
    return jnp.sum((jnp.cumsum(member, axis=0) - member) * member, axis=1)


def fill_table(w_ref, wv_ref):
    for idx in range(wv_ref.shape[0]):
        wv_ref[idx] = jnp.full(wv_ref.shape[1:], w_ref[idx], jnp.float32)


def primal_kernel(full, hid, rows, nlo, outs, w_ref, f_ref, *refs):
    if full:
        s_ref, b_ref, lob_ref, hib_ref = refs[:4]
    else:
        b_ref, lob_ref, hib_ref = refs[:3]
    o_ref = refs[-2]
    wv_ref = refs[-1]
    first_step = (pl.program_id(0) == 0) & (pl.program_id(1) == 0)
    pl.when(first_step)(functools.partial(fill_table, w_ref, wv_ref))
    nz = b_ref.shape[0]
    yb = b_ref.shape[1]
    nx = b_ref.shape[2]
    nin = CH + 1
    bias_at = 3 * hid * nin
    mix_at = bias_at + hid
    halves = [(r, pl.ds(k * 128, 128)) for r in range(0, rows, 8) for k in range(nx // 128)]
    step = pl.program_id(1)

    def plane(zz, c, ys, xs):
        if c == CH:
            if zz < 0:
                return lob_ref[zz + nlo, pl.ds(ys, 8), xs]
            if zz >= nz:
                return hib_ref[zz - nz, pl.ds(ys, 8), xs]
            return b_ref[zz, pl.ds(ys, 8), xs]
        return s_ref[zz + 1, c, pl.ds(ys, 8), xs]

    def weight(idx):
        return wv_ref[idx]

    chans = list(range(CH + 1)) if full else [CH]

    def one_plane(z):
        def body(i, carry):
            ys = pl.multiple_of(i * rows, rows)
            taps = [(t, c) for t in range(3) for c in chans]
            change = [[None] * len(halves) for _ in range(CH)]
            group = 4 if full else hid
            for first in range(0, hid, group):
                members = range(first, first + group)
                acc = {h: [weight(bias_at + h)] * len(halves) for h in members}
                for t, c in taps:
                    values = [plane(z + t - 1, c, ys + r, xs) for r, xs in halves]
                    for h in members:
                        w = weight((t * hid + h) * nin + c)
                        acc[h] = [a + w * v for a, v in zip(acc[h], values)]
                for h in members:
                    hidden = [jnp.maximum(a, 0.0) for a in acc[h]]
                    for c in range(CH):
                        w = weight(mix_at + c * hid + h)
                        change[c] = [
                            w * a if old is None else old + w * a
                            for old, a in zip(change[c], hidden)
                        ]
            for c in range(CH):
                for k, (r, xs) in enumerate(halves):
                    if full:
                        out = s_ref[z + 1, c, pl.ds(ys + r, 8), xs] + change[c][k]
                    elif z < 0:
                        out = change[c][k] * f_ref[0]
                    elif z >= nz:
                        out = change[c][k] * f_ref[1]
                    else:
                        out = change[c][k]
                    o_ref[0, c, pl.ds(ys + r, 8), xs] = out
            return carry

        lax.fori_loop(0, yb // rows, body, 0)

    for idx, z in enumerate(outs):
        pl.when(step == idx)(functools.partial(one_plane, z))


def primal_part(state, back, lo_b, hi_b, flags, wv, hid, outs, slot_of, total, into):
    nz, ny, nx = back.shape
    nlo = lo_b.shape[0]
    full = state is not None
    rows = 16
    smem = pl.BlockSpec(memory_space=pltpu.SMEM)
    spec_s = pl.BlockSpec((nz + 2, CH, YB, nx), lambda j, k: (0, 0, j, 0))
    spec_b = pl.BlockSpec((nz, YB, nx), lambda j, k: (0, j, 0))
    spec_h = pl.BlockSpec((nlo, YB, nx), lambda j, k: (0, j, 0))
    spec_o = pl.BlockSpec((1, CH, YB, nx), lambda j, k: (slot_of(k), 0, j, 0))
    operands = (back, lo_b, hi_b)
    specs = [spec_b, spec_h, spec_h]
    if full:
        operands = (state,) + operands
        specs = [spec_s] + specs
    aliases = {}
    if into is not None:
        aliases = {2 + len(operands): 0}
        operands = operands + (into,)
        specs = specs + [pl.BlockSpec(memory_space=pl.ANY)]
    return pl.pallas_call(
        functools.partial(primal_kernel, full, hid, rows, nlo, outs),
        grid=(ny // YB, len(outs)),
        in_specs=[smem, smem] + specs,
        out_specs=spec_o,
        out_shape=jax.ShapeDtypeStruct((total, CH, ny, nx), jnp.float32),
        scratch_shapes=[pltpu.VMEM((wv.shape[0], 8, 128), jnp.float32)],
        input_output_aliases=aliases,
        compiler_params=pltpu.CompilerParams(dimension_semantics=("arbitrary", "arbitrary")),
    )(wv, flags, *operands)


def weight_vectors(w1, b1, w2):
    return jnp.concatenate([w1.reshape(-1), b1, w2.reshape(-1)])


def dual_kernel(full, hid, w_ref, f_ref, *refs):
    if full:
        s_ref, p_ref, m_ref, o_ref, wv_ref = refs
        outs = range(o_ref.shape[0])
    else:
        m_ref, o_ref, wv_ref = refs
        outs = range(-1, o_ref.shape[0] - 1)
    nv = m_ref.shape[0] - 4
    nin = CH + 2
    fill_table(w_ref, wv_ref)
    bias_at = 3 * hid * nin
    mix_at = bias_at + hid

    def weight(idx):
        return jnp.concatenate([wv_ref[idx]] * 2, axis=0)

    def plane(zz, c):
        if c == CH + 1:
            return m_ref[zz + 2]
        if c == CH:
            return p_ref[zz + 1]
        return s_ref[zz + 1, c]

    chans = list(range(CH + 2)) if full else [CH + 1]
    for slot, z in enumerate(outs):
        inputs = [(t, c, plane(z + t - 1, c)) for t in range(3) for c in chans]
        change = [None] * CH
        for h in range(hid):
            acc = None
            for t, c, value in inputs:
                term = weight((t * hid + h) * nin + c) * value
                acc = term if acc is None else acc + term
            acc = jnp.maximum(acc + weight(bias_at + h), 0.0)
            for c in range(CH):
                term = weight(mix_at + c * hid + h) * acc
                change[c] = term if change[c] is None else change[c] + term
        for c in range(CH):
            if full:
                out = s_ref[z + 1, c] + change[c]
            elif z < 0:
                out = change[c] * f_ref[0]
            elif z >= nv:
                out = change[c] * f_ref[1]
            else:
                out = change[c]
            o_ref[slot, c] = out


def dual_step(state, projected, measured_ext, flags, w1, b1, w2):
    nv = measured_ext.shape[0] - 4
    _, rows, cols = measured_ext.shape
    hid = b1.shape[0]
    full = state is not None
    outs = nv if full else nv + 2
    smem = pl.BlockSpec(memory_space=pltpu.SMEM)
    vmem = pl.BlockSpec(memory_space=pltpu.VMEM)
    operands = (state, projected, measured_ext) if full else (measured_ext,)
    packed = weight_vectors(w1, b1, w2)
    return pl.pallas_call(
        functools.partial(dual_kernel, full, hid),
        in_specs=[smem, smem] + [vmem] * len(operands),
        out_specs=vmem,
        out_shape=jax.ShapeDtypeStruct((outs, CH, rows, cols), jnp.float32),
        scratch_shapes=[pltpu.VMEM((packed.shape[0], 8, cols), jnp.float32)],
    )(packed, flags, *operands)


def local(
    measured,
    bank,
    owner_tile,
    line_index,
    block_index,
    dual_w1,
    dual_b1,
    dual_w2,
    primal_w1,
    primal_b1,
    primal_w2,
):
    view_dev, drow_dev, dcols = measured.shape
    blocks = bank.shape[0]
    width = bank.shape[2]
    per_row = owner_tile.shape[2]
    angle_count = lax.axis_size("angle")
    row_count = lax.axis_size("row")
    owners = angle_count * row_count
    ray_rows = view_dev * drow_dev
    pair_count = ray_rows * per_row
    capacity = 2 * pair_count // owners
    slots = owners * capacity
    lines_dev = SLAB_DEV * NY
    both = ("angle", "row")
    owner_flat = owner_tile.reshape(-1)
    line_flat = line_index.reshape(-1)
    block_flat = block_index.reshape(-1)
    slot_flat = exclusive_slots(owner_flat, owners)
    dest = owner_flat * capacity + slot_flat
    pair_ids = jnp.arange(pair_count, dtype=jnp.int32)
    row_block = (pair_ids // per_row) * blocks + block_flat

    slot_ids = jnp.arange(slots, dtype=jnp.int32)
    hit = dest[None, :] == slot_ids[:, None]
    ids_send = jnp.sum(jnp.where(hit, line_flat[None, :] + 1, 0), axis=1) - 1
    slot_rb = jnp.sum(jnp.where(hit, row_block[None, :] + 1, 0), axis=1) - 1
    gsel = (
        slot_rb[None, :] == jnp.arange(ray_rows * blocks, dtype=jnp.int32)[:, None]
    ).astype(jnp.bfloat16)
    coded = (ids_send + 1).reshape(owners, capacity)
    code_row = jnp.concatenate(
        [coded // 32, coded % 32, jnp.zeros((owners, width - 2 * capacity), jnp.int32)], axis=1
    ).astype(jnp.bfloat16)[:, None, :]
    selectors = {}

    def line_selectors(arrived_codes):
        codes = arrived_codes.astype(jnp.int32)
        arrived_ids = (codes[:, :capacity] * 32 + codes[:, capacity : 2 * capacity] - 1).reshape(-1)
        selectors["rsel"] = (
            arrived_ids[:, None] == jnp.arange(lines_dev, dtype=jnp.int32)[None, :]
        ).astype(jnp.bfloat16)
        selectors["rsel_t"] = (
            arrived_ids[None, :] == jnp.arange(lines_dev, dtype=jnp.int32)[:, None]
        ).astype(jnp.bfloat16)
    place = lax.axis_index(both)
    flags = jnp.stack([place > 0, place < owners - 1]).astype(jnp.float32)

    flat_bank = jnp.transpose(bank, (1, 0, 2)).reshape(dcols, blocks * width)
    bank_t = jnp.transpose(bank, (0, 2, 1)).reshape(blocks * width, dcols).astype(jnp.float32)

    def forward(volume_lines):
        chosen = jnp.dot(selectors["rsel"], volume_lines, preferred_element_type=jnp.float32).astype(
            jnp.bfloat16
        )
        returned = lax.all_to_all(
            chosen.reshape(owners, capacity, width), both, split_axis=0, concat_axis=0, tiled=True
        ).reshape(slots, width)
        summed = jnp.dot(gsel, returned, preferred_element_type=jnp.float32)
        rays = jnp.dot(
            summed.reshape(ray_rows, blocks * width), bank_t, precision=highest
        )
        return rays.reshape(view_dev, drow_dev, dcols)

    def backward(sino_rows):
        all_blocks = jnp.dot(sino_rows, flat_bank, preferred_element_type=jnp.float32).astype(
            jnp.bfloat16
        )
        outgoing = lax.dot_general(
            gsel,
            all_blocks.reshape(ray_rows * blocks, width),
            (((0,), (0,)), ((), ())),
            preferred_element_type=jnp.float32,
        ).astype(jnp.bfloat16)
        outgoing = outgoing.reshape(owners, capacity, width)
        if not selectors:
            outgoing = jnp.concatenate([outgoing, code_row], axis=1)
        arrived = lax.all_to_all(outgoing, both, split_axis=0, concat_axis=0, tiled=True)
        if not selectors:
            line_selectors(arrived[:, capacity, :])
            arrived = arrived[:, :capacity]
        arrived = arrived.reshape(slots, width)
        back = jnp.dot(selectors["rsel_t"], arrived, preferred_element_type=jnp.float32)
        return back.reshape(SLAB_DEV, NY, width)

    angle_place = lax.axis_index("angle")
    view_flags = jnp.stack([angle_place > 0, angle_place < angle_count - 1]).astype(jnp.float32)
    lo_m, hi_m = shift_pair(measured[-2:], measured[:2], "angle")
    measured_ext = jnp.concatenate([lo_m, measured, hi_m], axis=0)
    dual = None
    state = None
    for iteration in range(ITERS):
        if iteration == 0:
            dual = dual_step(
                None, None, measured_ext, view_flags,
                dual_w1[iteration], dual_b1[iteration], dual_w2[iteration],
            )
        else:
            volume_lines = state[1:-1, 1].reshape(lines_dev, width).astype(jnp.bfloat16)
            projected = forward(volume_lines)
            lo_p, hi_p = shift_pair(projected[-1:], projected[:1], "angle")
            projected_ext = jnp.concatenate([lo_p, projected, hi_p], axis=0)
            dual = dual_step(
                dual, projected_ext, measured_ext, view_flags,
                dual_w1[iteration], dual_b1[iteration], dual_w2[iteration],
            )
        core = dual if iteration > 0 else dual[1:-1]
        sino_rows = core[:, 0].reshape(ray_rows, dcols).astype(jnp.bfloat16)
        back = backward(sino_rows)
        wv = weight_vectors(primal_w1[iteration], primal_b1[iteration], primal_w2[iteration])
        hid = primal_b1.shape[1]
        nz = back.shape[0]
        if state is None:
            lo_b, hi_b = shift_pair(back[-2:], back[:2], both)
            inner = primal_part(
                None, back, back[:2], back[:2], flags, wv, hid,
                (1, 2), lambda k: k + 2, nz + 2, None,
            )
            state = primal_part(
                None, back, lo_b, hi_b, flags, wv, hid,
                (-1, 0, nz - 1, nz), lambda k: k + (k // 2) * 2, nz + 2, inner,
            )
        else:
            lo_b, hi_b = shift_pair(back[-1:], back[:1], both)
            inner = primal_part(
                state, back, back[:1], back[:1], flags, wv, hid,
                (1, 2), lambda k: k + 1, nz, None,
            )
            state = primal_part(
                state, back, lo_b, hi_b, flags, wv, hid,
                (0, nz - 1), lambda k: k * 3, nz, inner,
            )
    primal_state = jnp.transpose(state, (0, 2, 1, 3))
    dual_state = jnp.transpose(dual, (0, 2, 1, 3))
    return (primal_state, dual_state)


def solution(mesh):
    placed = (
        P("angle", "row", None),
        P(),
        P(("angle", "row"), None, None),
        P(("angle", "row"), None, None),
        P(("angle", "row"), None, None),
        P(),
        P(),
        P(),
        P(),
        P(),
        P(),
    )
    return jax.shard_map(
        local,
        mesh=mesh,
        in_specs=placed,
        out_specs=(P(("angle", "row"), None, None, None), P("angle", "row", None, None)),
        check_vma=False,
    )
```
